256 devices in a mesh: seq: 64 (over z, y_lo, x), tp: 4 (over y_hi, core).
Axes of the slice: x: 4, y: 4 (y_hi: 2, y_lo: 2; y = y_hi * 2 + y_lo), z: 8, core: 2. Of those that a mesh axis runs over, the one named last changes fastest.
Arguments:
- tokens: bfloat16 [16384, 2560], P('seq', 'tp'), may hold values from -24 to 24
- norm_gain: bfloat16 [2560], replicated, may hold values from 0.099609375 to 1.8984375
- w_query: bfloat16 [2560, 2560], P(None, 'tp'), may hold values from -0.25 to 0.25
- w_key: bfloat16 [2560, 640], P(None, 'tp'), may hold values from -0.125 to 0.125
- w_value: bfloat16 [2560, 640], P(None, 'tp'), may hold values from -0.125 to 0.125
- w_out: bfloat16 [2560, 2560], P('tp'), may hold values from -0.625 to 0.625
- kv_pool: bfloat16 [1152, 2, 8, 80, 128], P('seq', None, 'tp'), may hold values from -32 to 32
- cache_lengths: int32 [16], replicated, may hold values from 128 to 8192, as said below
- page_table: int32 [16, 72], replicated, may hold values from 0 to 17, as said below
Outputs:
- hidden: bfloat16 [16384, 2560], P('seq', 'tp')
- new_pool: bfloat16 [1152, 2, 8, 80, 128], P('seq', None, 'tp')
The draws below stay inside these ranges and needn't reach their ends.
Inputs may be any that keep to these rules, and one draw needn't show every extreme that they name: `cache_lengths`: multiples of 128; some group has exactly 8192 and some exactly 128. Group g is the indices g * 4 to g * 4 + 3 of seq. Logical page q of group g (cached or new) lies on member q mod 4 of the group, in local slot page_table[g, q] of that device's 18 slots of kv_pool; for each group and member the 18 logical pages of that member take all 18 slots once.
All inputs are finite; a program needn't handle non-finite values.
Results may differ from the reference program's by a relative error of at most 0.017.
Values may be sent and summed in bfloat16 or wider, within the bound.
No kernel may reach another device: no remote copies, remote signals or barrier semaphores. Data moves between devices by JAX's collectives and lax.ppermute only.
A program may use at most 128 MiB of HBM per device.

```python
import math
import jax
import jax.numpy as jnp
from jax import lax

D = 2560
H = 32
KVH = 8
HD = 80
PAGE = 128
MAXLEN = 8192
GROUP = 4
NEW_TOK = 1024
REQS = 16
TOKENS = 16384
OLD_PAGES = 64
NEW_PAGES = 8
MAX_PAGES = 72
PAGES_DEV = 18
PAGES = 1152
N_TP = 4


def draw_tokens(key, part):
    first_key, second_key, third_key = jax.random.split(key, 3)
    row_scale = jnp.exp(jax.random.uniform(first_key, (TOKENS, 1), minval=math.log(0.5), maxval=math.log(2.0)))
    col_scale = jnp.exp(jax.random.uniform(second_key, (1, D), minval=math.log(0.5), maxval=math.log(2.0)))
    base_values = jnp.clip(jax.random.normal(third_key, (TOKENS, D)), -6.0, 6.0)
    return (base_values * row_scale * col_scale).astype(jnp.bfloat16)


def draw_kv_pool(key, part):
    first_key = jax.random.fold_in(key, 0)
    shape = (PAGES, 2, KVH, HD, PAGE)
    base_values = jnp.clip(jax.random.normal(first_key, shape), -6.0, 6.0)
    return base_values.astype(jnp.bfloat16)


def draw_cache_lengths(key, part):
    first_key, second_key = jax.random.split(jax.random.fold_in(key, 11), 2)
    page_counts = jax.random.randint(first_key, (REQS,), 1, MAXLEN // PAGE + 1)
    ordering = jax.random.permutation(second_key, REQS)
    page_counts = page_counts.at[ordering[0]].set(MAXLEN // PAGE).at[ordering[1]].set(1)
    return (page_counts * PAGE).astype(jnp.int32)


def draw_page_table(key, part):
    row_keys = jax.random.split(jax.random.fold_in(key, 23), REQS * GROUP)
    orders = jax.vmap(lambda row_key: jax.random.permutation(row_key, PAGES_DEV))(row_keys)
    return orders.reshape(REQS, GROUP, PAGES_DEV).transpose(0, 2, 1).reshape(REQS, MAX_PAGES).astype(jnp.int32)


def level_of(stream_key, dims, cuts, smallest, top_value):
    gain, own = 1.0, jax.random.fold_in(stream_key, 6)
    for axis_at, parts in cuts:
        heights = jnp.exp(jax.random.uniform(jax.random.fold_in(own, axis_at), (parts,), jnp.float32, smallest / len(cuts), top_value / len(cuts)))
        gain = gain * jnp.repeat(heights, dims[axis_at] // parts).reshape([-1 if axis == axis_at else 1 for axis in range(len(dims))])
    return gain


def gaussian(own_key, extent, width, bound, shards=(), held_as=jnp.bfloat16):
    array = width * jax.random.normal(own_key, extent, jnp.float32)
    if shards:
        array = array * level_of(own_key, extent, shards, -0.22, 0.18)
    return jnp.clip(array, -bound, bound).astype(held_as)


def setup_inputs(seed: int = 0) -> dict:
    splits = jax.random.split(jax.random.key(seed), 10)
    tokens = draw_tokens(jax.random.fold_in(splits[9], 71), 0)
    norm_gain = jnp.clip(1.0 + 0.18 * jax.random.normal(splits[1], (D,), jnp.float32), 0.099609375, 1.8984375).astype(jnp.bfloat16)
    w_query = gaussian(splits[2], (D, H * HD), (D // 4) ** -0.5, 0.25, ((1, 4),))
    w_key = gaussian(splits[3], (D, KVH * HD), D ** -0.5, 0.125, ((1, 4),))
    w_value = gaussian(splits[4], (D, KVH * HD), D ** -0.5, 0.125, ((1, 4),))
    w_out = gaussian(splits[5], (H * HD, D), HD ** -0.5, 0.625, ((0, 4),))
    kv_pool = draw_kv_pool(jax.random.fold_in(splits[9], 71), 0)
    cache_lengths = draw_cache_lengths(jax.random.fold_in(splits[9], 71), 0)
    page_table = draw_page_table(jax.random.fold_in(splits[9], 71), 0)
    return dict(tokens=tokens, norm_gain=norm_gain, w_query=w_query, w_key=w_key, w_value=w_value, w_out=w_out, kv_pool=kv_pool, cache_lengths=cache_lengths, page_table=page_table)


norm_eps = 1e-05
rope_base = 1000000.0
masked_score = -1e+30

def rotate(values, positions):
    head_dim = values.shape[-1]
    half_dim = head_dim // 2
    frequency = rope_base ** (-(jnp.arange(half_dim, dtype=jnp.float32) * 2.0) / head_dim)
    angles = positions.astype(jnp.float32)[:, None] * frequency[None, :]
    cosine = jnp.cos(angles)[:, None, :]
    sine_part = jnp.sin(angles)[:, None, :]
    first_half = values[..., :half_dim]
    second_half = values[..., half_dim:]
    return jnp.concatenate([first_half * cosine - second_half * sine_part, second_half * cosine + first_half * sine_part], axis=-1)

def reference(tokens, norm_gain, w_query, w_key, w_value, w_out, kv_pool, cache_lengths, page_table):
    rows_float = tokens.astype(jnp.float32)
    normed = (rows_float * lax.rsqrt(lax.optimization_barrier(jnp.mean(rows_float * rows_float, axis=-1, keepdims=True)) + norm_eps) * norm_gain.astype(jnp.float32)).astype(jnp.bfloat16)
    query_all = jnp.dot(normed, w_query, preferred_element_type=jnp.float32)
    key_all = jnp.dot(normed, w_key, preferred_element_type=jnp.float32)
    value_all = jnp.dot(normed, w_value, preferred_element_type=jnp.float32).astype(jnp.bfloat16)
    pool_groups = kv_pool.reshape((REQS, GROUP * PAGES_DEV) + kv_pool.shape[1:])
    group_size = H // KVH

    def one_group(group_id):
        length = cache_lengths[group_id]
        first_new = length // PAGE
        table_row = page_table[group_id]
        start = (group_id * NEW_TOK).astype(jnp.int32)
        positions = length + jnp.arange(NEW_TOK, dtype=jnp.int32)
        query = rotate(lax.dynamic_slice_in_dim(query_all, start, NEW_TOK, 0).reshape(NEW_TOK, H, HD), positions).astype(jnp.bfloat16)
        new_keys = rotate(lax.dynamic_slice_in_dim(key_all, start, NEW_TOK, 0).reshape(NEW_TOK, KVH, HD), positions).astype(jnp.bfloat16)
        new_values = lax.dynamic_slice_in_dim(value_all, start, NEW_TOK, 0).reshape(NEW_TOK, KVH, HD)
        pool_group = pool_groups[group_id]
        logical = jnp.arange(OLD_PAGES, dtype=jnp.int32)
        cached = pool_group[logical % GROUP * PAGES_DEV + table_row[:OLD_PAGES]]
        cache_keys = cached[:, 0].transpose(1, 2, 0, 3).reshape(KVH, HD, MAXLEN)
        cache_values = cached[:, 1].transpose(1, 2, 0, 3).reshape(KVH, HD, MAXLEN)
        keys_all = jnp.concatenate([cache_keys, new_keys.transpose(1, 2, 0)], axis=2).astype(jnp.float32)
        values_all = jnp.concatenate([cache_values, new_values.transpose(1, 2, 0)], axis=2).astype(jnp.float32)
        key_pos = jnp.arange(MAXLEN + NEW_TOK, dtype=jnp.int32)
        query_pos = jnp.arange(NEW_TOK, dtype=jnp.int32)
        valid = jnp.where(key_pos[None, :] < MAXLEN, (key_pos < length)[None, :], key_pos[None, :] - MAXLEN <= query_pos[:, None])
        query_heads = lax.optimization_barrier(query).astype(jnp.float32).reshape(NEW_TOK, KVH, group_size, HD)

        def one_head(head_id):
            query_head = lax.dynamic_index_in_dim(query_heads, head_id, 1, keepdims=False)
            scores = jnp.einsum('tgd,dn->tgn', query_head, keys_all[head_id]) * HD ** (-0.5)
            scores = jnp.where(valid[:, None, :], scores, masked_score)
            top_score = lax.optimization_barrier(jnp.max(scores, axis=-1, keepdims=True))
            weights = jnp.where(valid[:, None, :], jnp.exp(scores - top_score), 0.0)
            weight_sum = lax.optimization_barrier(jnp.sum(weights, axis=-1))
            rounded = lax.optimization_barrier(weights.astype(jnp.bfloat16)).astype(jnp.float32)
            return jnp.einsum('tgn,dn->tgd', rounded, values_all[head_id]) / weight_sum[..., None]
        heads_out = lax.map(one_head, jnp.arange(KVH, dtype=jnp.int32))
        attended = heads_out.transpose(1, 0, 2, 3).reshape(NEW_TOK, H * HD).astype(jnp.bfloat16)
        key_pages = new_keys.reshape(NEW_PAGES, PAGE, KVH, HD).transpose(0, 2, 3, 1)
        value_pages = new_values.reshape(NEW_PAGES, PAGE, KVH, HD).transpose(0, 2, 3, 1)
        new_pages = jnp.stack([key_pages, value_pages], axis=1)
        logical_new = first_new + jnp.arange(NEW_PAGES, dtype=jnp.int32)
        new_rows = logical_new % GROUP * PAGES_DEV + table_row[logical_new]
        pool_group = pool_group.at[new_rows].set(new_pages)
        return (attended, pool_group)
    attended_all, pools = lax.map(one_group, jnp.arange(REQS, dtype=jnp.int32))
    attended_all = attended_all.reshape(TOKENS, H * HD)
    per_shard = H * HD // N_TP
    summed = jnp.zeros((TOKENS, D), jnp.float32)
    for shard_id in range(N_TP):
        term = jnp.dot(attended_all[:, shard_id * per_shard:(shard_id + 1) * per_shard], w_out[shard_id * per_shard:(shard_id + 1) * per_shard], preferred_element_type=jnp.float32)
        summed = summed + lax.optimization_barrier(term.astype(jnp.bfloat16)).astype(jnp.float32)
    hidden = (rows_float + summed).astype(jnp.bfloat16)
    return (hidden, pools.reshape(kv_pool.shape))
```

```python
import functools

import jax
import jax.numpy as jnp
from jax import lax
from jax.experimental import pallas as pl
from jax.experimental.pallas import tpu as pltpu
from jax.sharding import PartitionSpec as P

HD = 80
PAGE = 128
MAXLEN = 8192
GROUP = 4
PAGES_PER_STEP = 8


norm_eps = 1e-05
rope_base = 1000000.0
masked_score = -1e30


def rotate(values, positions):
    head_dim = values.shape[-1]
    half_dim = head_dim // 2
    frequency = rope_base ** (-(jnp.arange(half_dim, dtype=jnp.float32) * 2.0) / head_dim)
    angles = positions.astype(jnp.float32)[:, None] * frequency[None, :]
    cosine = jnp.cos(angles)[:, None, :]
    sine_part = jnp.sin(angles)[:, None, :]
    first_half = values[..., :half_dim]
    second_half = values[..., half_dim:]
    return jnp.concatenate(
        [
            first_half * cosine - second_half * sine_part,
            second_half * cosine + first_half * sine_part,
        ],
        axis=-1,
    )


def group_shift(x, axis, shift):
    size = lax.axis_size(axis)
    pairs = [(i, i - i % GROUP + (i % GROUP + shift) % GROUP) for i in range(size)]
    return lax.ppermute(x, axis, pairs)


def partial_kernel(
    slots_ref, meta_ref, q_ref, *rest, pages_per_step, cached_steps, rows_per_tok, tok_count, scale
):
    pool_refs = rest[:pages_per_step]
    fresh_ref = rest[pages_per_step]
    o_ref, lse_ref = rest[pages_per_step + 1 : pages_per_step + 3]
    m_sc, l_sc, acc_sc = rest[pages_per_step + 3 :]
    block = pl.program_id(1)
    step = pl.program_id(2)
    cached_count = meta_ref[0]
    member = meta_ref[1]
    source = (member - block + GROUP) % GROUP

    @pl.when(step == 0)
    def _():
        m_sc[...] = jnp.full(m_sc.shape, masked_score, jnp.float32)
        l_sc[...] = jnp.zeros(l_sc.shape, jnp.float32)
        acc_sc[...] = jnp.zeros(acc_sc.shape, jnp.float32)

    def update(kv_pairs, masks):
        q = q_ref[...]
        scores = []
        for (k, _), mask in zip(kv_pairs, masks):
            s = lax.dot_general(q, k, (((1,), (0,)), ((), ())), preferred_element_type=jnp.float32)
            if mask is not None:
                s = jnp.where(mask, s, masked_score)
            scores.append(s)
        m_prev = m_sc[...]
        m_new = m_prev
        for s in scores:
            m_new = jnp.maximum(m_new, jnp.max(s, axis=1, keepdims=True))
        alpha = jnp.exp((m_prev - m_new) * scale)
        l_new = alpha * l_sc[...]
        acc = alpha * acc_sc[...]
        for s, (_, v), mask in zip(scores, kv_pairs, masks):
            p = jnp.exp((s - m_new) * scale)
            if mask is not None:
                p = jnp.where(mask, p, 0.0)
            l_new = l_new + jnp.sum(p, axis=1, keepdims=True)
            acc = acc + lax.dot_general(
                p.astype(jnp.bfloat16), v, (((1,), (1,)), ((), ())), preferred_element_type=jnp.float32
            )
        m_sc[...] = m_new
        l_sc[...] = l_new
        acc_sc[...] = acc

    cached_pairs = [(ref[0], ref[1]) for ref in pool_refs]
    first_page = step * pages_per_step
    is_cached = step < cached_steps

    @pl.when(is_cached & (first_page + pages_per_step <= cached_count))
    def _():
        update(cached_pairs, [None] * pages_per_step)

    @pl.when(is_cached & (first_page < cached_count) & (first_page + pages_per_step > cached_count))
    def _():
        update(cached_pairs, [first_page + i < cached_count for i in range(pages_per_step)])

    fresh_pages = fresh_ref.shape[0]
    fresh_pairs = [(fresh_ref[e, 0], fresh_ref[e, 1]) for e in range(fresh_pages)]
    is_fresh = step == cached_steps

    @pl.when(is_fresh & (source > member))
    def _():
        update(fresh_pairs, [None] * fresh_pages)

    @pl.when(is_fresh & (source == member))
    def _():
        rows = q_ref.shape[0]
        row_tok = lax.broadcasted_iota(jnp.int32, (rows, PAGE), 0) // rows_per_tok
        col = lax.broadcasted_iota(jnp.int32, (rows, PAGE), 1)
        masks = [e * PAGE + col <= row_tok for e in range(fresh_pages)]
        update(fresh_pairs, masks)

    @pl.when(is_fresh)
    def _():
        total = l_sc[...]
        filled = total > 0.0
        safe = jnp.where(filled, total, 1.0)
        o_ref[...] = (acc_sc[...] / safe).astype(o_ref.dtype)
        lse_ref[...] = jnp.where(filled, m_sc[...] * scale + jnp.log(safe), masked_score)


def partial_attention(q_all, kv_pool, fresh, slots, meta, cached_steps):
    blocks, kv_heads, rows, head_dim = q_all.shape
    pages_per_step = PAGES_PER_STEP
    fresh_pages = fresh.shape[0]
    tok_count = fresh_pages * PAGE
    rows_per_tok = rows // tok_count
    scale = head_dim ** (-0.5)

    def pool_map(i):
        def index_map(h, b, j, slots_ref, meta_ref):
            jj = jnp.minimum(j, cached_steps - 1)
            idx = jnp.minimum(jj * pages_per_step + i, jnp.maximum(meta_ref[0] - 1, 0))
            return (slots_ref[idx], 0, h, 0, 0)

        return index_map

    q_spec = pl.BlockSpec((None, None, rows, head_dim), lambda h, b, j, s, m: (b, h, 0, 0))
    pool_specs = [
        pl.BlockSpec((None, 2, None, head_dim, PAGE), pool_map(i)) for i in range(pages_per_step)
    ]
    fresh_spec = pl.BlockSpec(
        (fresh_pages, 2, None, head_dim, PAGE), lambda h, b, j, s, m: (0, 0, h, 0, 0)
    )
    o_spec = pl.BlockSpec((None, None, rows, head_dim), lambda h, b, j, s, m: (b, h, 0, 0))
    lse_spec = pl.BlockSpec((None, None, rows, 1), lambda h, b, j, s, m: (b, h, 0, 0))
    kernel = functools.partial(
        partial_kernel,
        pages_per_step=pages_per_step,
        cached_steps=cached_steps,
        rows_per_tok=rows_per_tok,
        tok_count=tok_count,
        scale=scale,
    )
    keys_per_row = cached_steps * pages_per_step * PAGE + tok_count
    cost = pl.CostEstimate(
        flops=4 * kv_heads * blocks * rows * keys_per_row * head_dim,
        transcendentals=kv_heads * blocks * rows * keys_per_row,
        bytes_accessed=2 * q_all.size * 3 + kv_heads * blocks * keys_per_row * head_dim * 4,
    )
    return pl.pallas_call(
        kernel,
        grid_spec=pltpu.PrefetchScalarGridSpec(
            num_scalar_prefetch=2,
            grid=(kv_heads, blocks, cached_steps + 1),
            in_specs=[q_spec] + pool_specs + [fresh_spec],
            out_specs=[o_spec, lse_spec],
            scratch_shapes=[
                pltpu.VMEM((rows, 1), jnp.float32),
                pltpu.VMEM((rows, 1), jnp.float32),
                pltpu.VMEM((rows, head_dim), jnp.float32),
            ],
        ),
        out_shape=[
            jax.ShapeDtypeStruct((blocks, kv_heads, rows, head_dim), jnp.bfloat16),
            jax.ShapeDtypeStruct((blocks, kv_heads, rows, 1), jnp.float32),
        ],
        compiler_params=pltpu.CompilerParams(
            dimension_semantics=("arbitrary", "arbitrary", "arbitrary")
        ),
        cost_estimate=cost,
    )(slots, meta, q_all, *([kv_pool] * pages_per_step), fresh)


def shards(tokens, norm_gain, w_query, w_key, w_value, w_out, kv_pool, cache_lengths, page_table):
    seq_position = lax.axis_index("seq")
    member = seq_position % GROUP
    group_id = seq_position // GROUP
    length = cache_lengths[group_id]
    first_new = length // PAGE
    table_row = page_table[group_id]
    tok_count = tokens.shape[0]
    kv_heads = w_key.shape[1] // HD
    q_heads = w_query.shape[1] // HD
    group_size = q_heads // kv_heads
    tok_pages = tok_count // PAGE
    cached_per_member = MAXLEN // PAGE // GROUP
    cached_steps = cached_per_member // PAGES_PER_STEP

    whole = lax.all_gather(tokens, "tp", axis=1, tiled=True)
    rows_float = whole.astype(jnp.float32)
    normed = (
        rows_float
        * lax.rsqrt(jnp.mean(rows_float * rows_float, axis=-1, keepdims=True) + norm_eps)
        * norm_gain.astype(jnp.float32)
    ).astype(jnp.bfloat16)
    positions = length + member * tok_count + jnp.arange(tok_count, dtype=jnp.int32)
    query_rows = jnp.dot(normed, w_query, preferred_element_type=jnp.float32).reshape(
        tok_count, q_heads, HD
    )
    query = (
        rotate(query_rows, positions)
        .astype(jnp.bfloat16)
        .reshape(tok_count, kv_heads, group_size, HD)
    )
    key_rows = jnp.dot(normed, w_key, preferred_element_type=jnp.float32).reshape(
        tok_count, kv_heads, HD
    )
    new_keys = rotate(key_rows, positions).astype(jnp.bfloat16)
    new_values = (
        jnp.dot(normed, w_value, preferred_element_type=jnp.float32)
        .astype(jnp.bfloat16)
        .reshape(tok_count, kv_heads, HD)
    )
    key_pages = new_keys.reshape(tok_pages, PAGE, kv_heads, HD).transpose(0, 2, 3, 1)
    value_pages = new_values.reshape(tok_pages, PAGE, kv_heads, HD).transpose(0, 2, 3, 1)
    fresh_local = jnp.stack([key_pages, value_pages], axis=1)

    q_own = query.transpose(1, 0, 2, 3).reshape(kv_heads, tok_count * group_size, HD)
    q_all = jnp.stack([q_own] + [group_shift(q_own, "seq", s) for s in range(1, GROUP)])
    fresh_all = [fresh_local] + [group_shift(fresh_local, "seq", s) for s in range(1, GROUP)]

    slots = table_row[member + GROUP * jnp.arange(cached_per_member, dtype=jnp.int32)]
    cached_count = jnp.maximum((first_new - member + GROUP - 1) // GROUP, 0)
    meta = jnp.stack([cached_count, member]).astype(jnp.int32)
    o_part, lse_part = partial_attention(q_all, kv_pool, fresh_local, slots, meta, cached_steps)

    o_list = [o_part[0]] + [group_shift(o_part[b], "seq", GROUP - b) for b in range(1, GROUP)]
    lse_list = [lse_part[0]] + [group_shift(lse_part[b], "seq", GROUP - b) for b in range(1, GROUP)]
    lse_top = lse_list[0]
    for x in lse_list[1:]:
        lse_top = jnp.maximum(lse_top, x)
    weights = [jnp.exp(x - lse_top) for x in lse_list]
    weight_total = weights[0]
    for w in weights[1:]:
        weight_total = weight_total + w
    combined = weights[0] * o_list[0].astype(jnp.float32)
    for w, o in zip(weights[1:], o_list[1:]):
        combined = combined + w * o.astype(jnp.float32)
    combined = combined / weight_total
    attended = (
        combined.reshape(kv_heads, tok_count, group_size, HD)
        .transpose(1, 0, 2, 3)
        .reshape(tok_count, q_heads * HD)
        .astype(jnp.bfloat16)
    )
    out_term = jnp.dot(attended, w_out, preferred_element_type=jnp.float32)
    summed = lax.psum_scatter(
        out_term.astype(jnp.bfloat16), "tp", scatter_dimension=1, tiled=True
    ).astype(jnp.float32)
    hidden = (tokens.astype(jnp.float32) + summed).astype(jnp.bfloat16)

    fresh_stack = jnp.stack(fresh_all)
    start_offset = (member - first_new) % GROUP
    new_pool = kv_pool
    for extra in range(2):
        page_id = start_offset + GROUP * extra
        source = page_id // tok_pages
        shift_id = (member - source) % GROUP
        page_piece = fresh_stack[shift_id, page_id % tok_pages]
        slot_id = table_row[first_new + page_id]
        new_pool = lax.dynamic_update_slice_in_dim(new_pool, page_piece[None], slot_id, 0)
    return (hidden, new_pool)


def solution(mesh):
    return jax.shard_map(
        shards,
        mesh=mesh,
        in_specs=(
            P("seq", "tp"),
            P(),
            P(None, "tp"),
            P(None, "tp"),
            P(None, "tp"),
            P("tp", None),
            P("seq", None, "tp", None, None),
            P(),
            P(),
        ),
        out_specs=(P("seq", "tp"), P("seq", None, "tp", None, None)),
        check_vma=False,
    )
```

```python
import functools

import jax
import jax.numpy as jnp
from jax import lax
from jax.experimental import pallas as pl
from jax.experimental.pallas import tpu as pltpu
from jax.sharding import PartitionSpec as P


HD = 80
PAGE = 128
MAXLEN = 8192
GROUP = 4
PAGES_PER_STEP = 8
BLOCK_ORDER = (0, 2, 1, 3)


norm_eps = 1e-05
rope_base = 1000000.0
masked_score = -1e30


def rotate(values, positions):
    head_dim = values.shape[-1]
    half_dim = head_dim // 2
    frequency = rope_base ** (-(jnp.arange(half_dim, dtype=jnp.float32) * 2.0) / head_dim)
    angles = positions.astype(jnp.float32)[:, None] * frequency[None, :]
    cosine = jnp.cos(angles)[:, None, :]
    sine_part = jnp.sin(angles)[:, None, :]
    first_half = values[..., :half_dim]
    second_half = values[..., half_dim:]
    return jnp.concatenate(
        [
            first_half * cosine - second_half * sine_part,
            second_half * cosine + first_half * sine_part,
        ],
        axis=-1,
    )


def group_shift(x, axis, shift):
    size = lax.axis_size(axis)
    pairs = [(i, i - i % GROUP + (i % GROUP + shift) % GROUP) for i in range(size)]
    return lax.ppermute(x, axis, pairs)


def partial_kernel(
    slots_ref, meta_ref, q_ref, *rest, pages_per_step, cached_steps, rows_per_tok, tok_count, scale
):
    pool_refs = rest[:pages_per_step]
    fresh_ref = rest[pages_per_step]
    o_ref, lse_ref = rest[pages_per_step + 1 : pages_per_step + 3]
    m_sc, l_sc, acc_sc = rest[pages_per_step + 3 :]
    step = pl.program_id(1)
    cached_count = meta_ref[0]
    member = meta_ref[1]
    source = meta_ref[2]

    @pl.when(step == 0)
    def _():
        m_sc[...] = jnp.full(m_sc.shape, masked_score, jnp.float32)
        l_sc[...] = jnp.zeros(l_sc.shape, jnp.float32)
        acc_sc[...] = jnp.zeros(acc_sc.shape, jnp.float32)

    def update(kv_pairs, page_flags, masks):
        q = q_ref[...]
        scores = []
        tops = []
        for (k, _), flag, mask in zip(kv_pairs, page_flags, masks):
            s = lax.dot_general(q, k, (((1,), (0,)), ((), ())), preferred_element_type=jnp.float32)
            if mask is not None:
                s = jnp.where(mask, s, masked_score)
            top = jnp.max(s, axis=1, keepdims=True)
            if flag is not None:
                top = jnp.where(flag, top, masked_score)
            scores.append(s)
            tops.append(top)
        m_prev = m_sc[...]
        m_new = m_prev
        for top in tops:
            m_new = jnp.maximum(m_new, top)
        alpha = jnp.exp((m_prev - m_new) * scale)
        l_new = alpha * l_sc[...]
        acc = alpha * acc_sc[...]
        for s, (_, v), flag, mask in zip(scores, kv_pairs, page_flags, masks):
            p = jnp.exp((s - m_new) * scale)
            if mask is not None:
                p = jnp.where(mask, p, 0.0)
            row_sum = jnp.sum(p, axis=1, keepdims=True)
            term = lax.dot_general(
                p.astype(jnp.bfloat16), v, (((1,), (1,)), ((), ())), preferred_element_type=jnp.float32
            )
            if flag is not None:
                row_sum = jnp.where(flag, row_sum, 0.0)
                term = jnp.where(flag, term, 0.0)
            l_new = l_new + row_sum
            acc = acc + term
        m_sc[...] = m_new
        l_sc[...] = l_new
        acc_sc[...] = acc

    cached_pairs = [(ref[0], ref[1]) for ref in pool_refs]
    first_page = step * pages_per_step

    @pl.when((step < cached_steps) & (first_page < cached_count))
    def _():
        flags = [first_page + i < cached_count for i in range(pages_per_step)]
        update(cached_pairs, flags, [None] * pages_per_step)

    fresh_pages = fresh_ref.shape[0]
    fresh_pairs = [(fresh_ref[e, 0], fresh_ref[e, 1]) for e in range(fresh_pages)]
    is_fresh = step == cached_steps

    @pl.when(is_fresh & (source >= member))
    def _():
        rows = q_ref.shape[0]
        row_tok = lax.broadcasted_iota(jnp.int32, (rows, PAGE), 0) // rows_per_tok
        col = lax.broadcasted_iota(jnp.int32, (rows, PAGE), 1)
        offset = (source - member) * tok_count
        masks = [e * PAGE + col <= row_tok + offset for e in range(fresh_pages)]
        update(fresh_pairs, [None] * fresh_pages, masks)

    @pl.when(is_fresh)
    def _():
        total = l_sc[...]
        filled = total > 0.0
        safe = jnp.where(filled, total, 1.0)
        o_ref[...] = (acc_sc[...] / safe).astype(o_ref.dtype)
        lse_ref[...] = jnp.where(filled, m_sc[...] * scale + jnp.log(safe), masked_score)


def partial_attention(q_block, kv_pool, fresh, slots, meta, cached_steps):
    kv_heads, rows, head_dim = q_block.shape
    pages_per_step = PAGES_PER_STEP
    fresh_pages = fresh.shape[0]
    tok_count = fresh_pages * PAGE
    rows_per_tok = rows // tok_count
    scale = head_dim ** (-0.5)

    def pool_map(i):
        def index_map(h, j, slots_ref, meta_ref):
            jj = jnp.minimum(j, cached_steps - 1)
            idx = jnp.minimum(jj * pages_per_step + i, jnp.maximum(meta_ref[0] - 1, 0))
            return (slots_ref[idx], 0, h, 0, 0)

        return index_map

    q_spec = pl.BlockSpec((None, rows, head_dim), lambda h, j, s, m: (h, 0, 0))
    pool_specs = [
        pl.BlockSpec((None, 2, None, head_dim, PAGE), pool_map(i)) for i in range(pages_per_step)
    ]
    fresh_spec = pl.BlockSpec(
        (fresh_pages, 2, None, head_dim, PAGE), lambda h, j, s, m: (0, 0, h, 0, 0)
    )
    o_spec = pl.BlockSpec((None, rows, head_dim), lambda h, j, s, m: (h, 0, 0))
    lse_spec = pl.BlockSpec((None, rows, 1), lambda h, j, s, m: (h, 0, 0))
    kernel = functools.partial(
        partial_kernel,
        pages_per_step=pages_per_step,
        cached_steps=cached_steps,
        rows_per_tok=rows_per_tok,
        tok_count=tok_count,
        scale=scale,
    )
    keys_per_row = cached_steps * pages_per_step * PAGE + tok_count
    cost = pl.CostEstimate(
        flops=4 * kv_heads * rows * keys_per_row * head_dim,
        transcendentals=kv_heads * rows * keys_per_row,
        bytes_accessed=2 * q_block.size * 3 + kv_heads * keys_per_row * head_dim * 4,
    )
    return pl.pallas_call(
        kernel,
        grid_spec=pltpu.PrefetchScalarGridSpec(
            num_scalar_prefetch=2,
            grid=(kv_heads, cached_steps + 1),
            in_specs=[q_spec] + pool_specs + [fresh_spec],
            out_specs=[o_spec, lse_spec],
            scratch_shapes=[
                pltpu.VMEM((rows, 1), jnp.float32),
                pltpu.VMEM((rows, 1), jnp.float32),
                pltpu.VMEM((rows, head_dim), jnp.float32),
            ],
        ),
        out_shape=[
            jax.ShapeDtypeStruct((kv_heads, rows, head_dim), jnp.bfloat16),
            jax.ShapeDtypeStruct((kv_heads, rows, 1), jnp.float32),
        ],
        compiler_params=pltpu.CompilerParams(dimension_semantics=("arbitrary", "arbitrary")),
        cost_estimate=cost,
    )(slots, meta, q_block, *([kv_pool] * pages_per_step), fresh)


def layer(tokens, norm_gain, w_query, w_key, w_value, w_out, kv_pool, cache_lengths, page_table):
    seq_position = lax.axis_index("seq")
    member = seq_position % GROUP
    group_id = seq_position // GROUP
    length = cache_lengths[group_id]
    first_new = length // PAGE
    table_row = page_table[group_id]
    tok_count = tokens.shape[0]
    kv_heads = w_key.shape[1] // HD
    q_heads = w_query.shape[1] // HD
    group_size = q_heads // kv_heads
    tok_pages = tok_count // PAGE
    cached_per_member = MAXLEN // PAGE // GROUP
    cached_steps = cached_per_member // PAGES_PER_STEP

    whole = lax.all_gather(tokens, "tp", axis=1, tiled=True)
    rows_float = whole.astype(jnp.float32)
    normed = (
        rows_float
        * lax.rsqrt(jnp.mean(rows_float * rows_float, axis=-1, keepdims=True) + norm_eps)
        * norm_gain.astype(jnp.float32)
    ).astype(jnp.bfloat16)
    positions = length + member * tok_count + jnp.arange(tok_count, dtype=jnp.int32)
    query_rows = jnp.dot(normed, w_query, preferred_element_type=jnp.float32).reshape(
        tok_count, q_heads, HD
    )
    query = (
        rotate(query_rows, positions)
        .astype(jnp.bfloat16)
        .reshape(tok_count, kv_heads, group_size, HD)
    )
    key_rows = jnp.dot(normed, w_key, preferred_element_type=jnp.float32).reshape(
        tok_count, kv_heads, HD
    )
    new_keys = rotate(key_rows, positions).astype(jnp.bfloat16)
    new_values = (
        jnp.dot(normed, w_value, preferred_element_type=jnp.float32)
        .astype(jnp.bfloat16)
        .reshape(tok_count, kv_heads, HD)
    )
    key_pages = new_keys.reshape(tok_pages, PAGE, kv_heads, HD).transpose(0, 2, 3, 1)
    value_pages = new_values.reshape(tok_pages, PAGE, kv_heads, HD).transpose(0, 2, 3, 1)
    fresh_local = jnp.stack([key_pages, value_pages], axis=1)

    q_own = query.transpose(1, 0, 2, 3).reshape(kv_heads, tok_count * group_size, HD)
    q_blocks = [q_own]
    for s in range(1, GROUP):
        q_blocks.append(group_shift(q_own, "seq", s))
    fresh_all = [fresh_local] + [group_shift(fresh_local, "seq", s) for s in range(1, GROUP)]

    slots = table_row[member + GROUP * jnp.arange(cached_per_member, dtype=jnp.int32)]
    cached_count = jnp.maximum((first_new - member + GROUP - 1) // GROUP, 0)
    o_list = [None] * GROUP
    lse_list = [None] * GROUP
    for b in BLOCK_ORDER:
        source = (member - b) % GROUP
        meta = jnp.stack([cached_count, member, source]).astype(jnp.int32)
        o_b, lse_b = partial_attention(q_blocks[b], kv_pool, fresh_local, slots, meta, cached_steps)
        if b:
            o_b = group_shift(o_b, "seq", GROUP - b)
            lse_b = group_shift(lse_b, "seq", GROUP - b)
        o_list[b] = o_b
        lse_list[b] = lse_b
    lse_top = lse_list[0]
    for x in lse_list[1:]:
        lse_top = jnp.maximum(lse_top, x)
    weights = [jnp.exp(x - lse_top) for x in lse_list]
    weight_total = weights[0]
    for w in weights[1:]:
        weight_total = weight_total + w
    combined = weights[0] * o_list[0].astype(jnp.float32)
    for w, o in zip(weights[1:], o_list[1:]):
        combined = combined + w * o.astype(jnp.float32)
    combined = combined / weight_total
    attended = (
        combined.reshape(kv_heads, tok_count, group_size, HD)
        .transpose(1, 0, 2, 3)
        .reshape(tok_count, q_heads * HD)
        .astype(jnp.bfloat16)
    )
    out_term = jnp.dot(attended, w_out, preferred_element_type=jnp.float32)
    summed = lax.psum_scatter(
        out_term.astype(jnp.bfloat16), "tp", scatter_dimension=1, tiled=True
    ).astype(jnp.float32)
    hidden = (tokens.astype(jnp.float32) + summed).astype(jnp.bfloat16)

    fresh_stack = jnp.stack(fresh_all)
    start_offset = (member - first_new) % GROUP
    new_pool = kv_pool
    for extra in range(2):
        page_id = start_offset + GROUP * extra
        source = page_id // tok_pages
        shift_id = (member - source) % GROUP
        page_piece = fresh_stack[shift_id, page_id % tok_pages]
        slot_id = table_row[first_new + page_id]
        new_pool = lax.dynamic_update_slice_in_dim(new_pool, page_piece[None], slot_id, 0)
    return (hidden, new_pool)


def solution(mesh):
    return jax.shard_map(
        layer,
        mesh=mesh,
        in_specs=(
            P("seq", "tp"),
            P(),
            P(None, "tp"),
            P(None, "tp"),
            P(None, "tp"),
            P("tp", None),
            P("seq", None, "tp", None, None),
            P(),
            P(),
        ),
        out_specs=(P("seq", "tp"), P("seq", None, "tp", None, None)),
        check_vma=False,
    )
```

```python
import functools

import jax
import jax.numpy as jnp
from jax import lax
from jax.experimental import pallas as pl
from jax.experimental.pallas import tpu as pltpu
from jax.sharding import PartitionSpec as P


HD = 80
PAGE = 128
MAXLEN = 8192
GROUP = 4
PAGES_PER_STEP = 8
BLOCK_ORDER = (0, 2, 1, 3)


norm_eps = 1e-05
rope_base = 1000000.0
masked_score = -1e30


def rotate(values, positions):
    head_dim = values.shape[-1]
    half_dim = head_dim // 2
    frequency = rope_base ** (-(jnp.arange(half_dim, dtype=jnp.float32) * 2.0) / head_dim)
    angles = positions.astype(jnp.float32)[:, None] * frequency[None, :]
    cosine = jnp.cos(angles)[:, None, :]
    sine_part = jnp.sin(angles)[:, None, :]
    first_half = values[..., :half_dim]
    second_half = values[..., half_dim:]
    return jnp.concatenate(
        [
            first_half * cosine - second_half * sine_part,
            second_half * cosine + first_half * sine_part,
        ],
        axis=-1,
    )


def group_shift(x, axis, shift):
    size = lax.axis_size(axis)
    pairs = [(i, i - i % GROUP + (i % GROUP + shift) % GROUP) for i in range(size)]
    return lax.ppermute(x, axis, pairs)


def tp_shift(x, shift):
    size = lax.axis_size("tp")
    return lax.ppermute(x, "tp", [(i, (i + shift) % size) for i in range(size)])


def partial_kernel(
    slots_ref, meta_ref, q_ref, *rest, pages_per_step, cached_steps, rows_per_tok, tok_count, scale
):
    pool_refs = rest[:pages_per_step]
    fresh_ref = rest[pages_per_step]
    o_ref, lse_ref = rest[pages_per_step + 1 : pages_per_step + 3]
    m_sc, l_sc, acc_sc = rest[pages_per_step + 3 :]
    step = pl.program_id(1)
    cached_count = meta_ref[0]
    member = meta_ref[1]
    source = meta_ref[2]

    @pl.when(step == 0)
    def _():
        m_sc[...] = jnp.full(m_sc.shape, masked_score, jnp.float32)
        l_sc[...] = jnp.zeros(l_sc.shape, jnp.float32)
        acc_sc[...] = jnp.zeros(acc_sc.shape, jnp.float32)

    def update(kv_pairs, page_flags, masks):
        q = q_ref[...]
        scores = []
        tops = []
        for (k, _), flag, mask in zip(kv_pairs, page_flags, masks):
            s = lax.dot_general(q, k, (((1,), (0,)), ((), ())), preferred_element_type=jnp.float32)
            if mask is not None:
                s = jnp.where(mask, s, masked_score)
            top = jnp.max(s, axis=1, keepdims=True)
            if flag is not None:
                top = jnp.where(flag, top, masked_score)
            scores.append(s)
            tops.append(top)
        m_prev = m_sc[...]
        m_new = m_prev
        for top in tops:
            m_new = jnp.maximum(m_new, top)
        alpha = jnp.exp((m_prev - m_new) * scale)
        l_new = alpha * l_sc[...]
        acc = alpha * acc_sc[...]
        for s, (_, v), flag, mask in zip(scores, kv_pairs, page_flags, masks):
            p = jnp.exp((s - m_new) * scale)
            if mask is not None:
                p = jnp.where(mask, p, 0.0)
            row_sum = jnp.sum(p, axis=1, keepdims=True)
            term = lax.dot_general(
                p.astype(jnp.bfloat16), v, (((1,), (1,)), ((), ())), preferred_element_type=jnp.float32
            )
            if flag is not None:
                row_sum = jnp.where(flag, row_sum, 0.0)
                term = jnp.where(flag, term, 0.0)
            l_new = l_new + row_sum
            acc = acc + term
        m_sc[...] = m_new
        l_sc[...] = l_new
        acc_sc[...] = acc

    cached_pairs = [(ref[0], ref[1]) for ref in pool_refs]
    first_page = step * pages_per_step

    @pl.when((step < cached_steps) & (first_page < cached_count))
    def _():
        flags = [first_page + i < cached_count for i in range(pages_per_step)]
        update(cached_pairs, flags, [None] * pages_per_step)

    fresh_pages = fresh_ref.shape[0]
    fresh_pairs = [(fresh_ref[e, 0], fresh_ref[e, 1]) for e in range(fresh_pages)]
    is_fresh = step == cached_steps

    @pl.when(is_fresh & (source >= member))
    def _():
        rows = q_ref.shape[0]
        row_tok = lax.broadcasted_iota(jnp.int32, (rows, PAGE), 0) // rows_per_tok
        col = lax.broadcasted_iota(jnp.int32, (rows, PAGE), 1)
        offset = (source - member) * tok_count
        masks = [e * PAGE + col <= row_tok + offset for e in range(fresh_pages)]
        update(fresh_pairs, [None] * fresh_pages, masks)

    @pl.when(is_fresh)
    def _():
        total = l_sc[...]
        filled = total > 0.0
        safe = jnp.where(filled, total, 1.0)
        o_ref[...] = (acc_sc[...] / safe).astype(o_ref.dtype)
        lse_ref[...] = jnp.where(filled, m_sc[...] * scale + jnp.log(safe), masked_score)


def partial_attention(q_block, kv_pool, fresh, slots, meta, cached_steps):
    kv_heads, rows, head_dim = q_block.shape
    pages_per_step = PAGES_PER_STEP
    fresh_pages = fresh.shape[0]
    tok_count = fresh_pages * PAGE
    rows_per_tok = rows // tok_count
    scale = head_dim ** (-0.5)

    def pool_map(i):
        def index_map(h, j, slots_ref, meta_ref):
            jj = jnp.minimum(j, cached_steps - 1)
            idx = jnp.minimum(jj * pages_per_step + i, jnp.maximum(meta_ref[0] - 1, 0))
            return (slots_ref[idx], 0, h, 0, 0)

        return index_map

    q_spec = pl.BlockSpec((None, rows, head_dim), lambda h, j, s, m: (h, 0, 0))
    pool_specs = [
        pl.BlockSpec((None, 2, None, head_dim, PAGE), pool_map(i)) for i in range(pages_per_step)
    ]
    fresh_spec = pl.BlockSpec(
        (fresh_pages, 2, None, head_dim, PAGE), lambda h, j, s, m: (0, 0, h, 0, 0)
    )
    o_spec = pl.BlockSpec((None, rows, head_dim), lambda h, j, s, m: (h, 0, 0))
    lse_spec = pl.BlockSpec((None, rows, 1), lambda h, j, s, m: (h, 0, 0))
    kernel = functools.partial(
        partial_kernel,
        pages_per_step=pages_per_step,
        cached_steps=cached_steps,
        rows_per_tok=rows_per_tok,
        tok_count=tok_count,
        scale=scale,
    )
    keys_per_row = cached_steps * pages_per_step * PAGE + tok_count
    cost = pl.CostEstimate(
        flops=4 * kv_heads * rows * keys_per_row * head_dim,
        transcendentals=kv_heads * rows * keys_per_row,
        bytes_accessed=2 * q_block.size * 3 + kv_heads * keys_per_row * head_dim * 4,
    )
    return pl.pallas_call(
        kernel,
        grid_spec=pltpu.PrefetchScalarGridSpec(
            num_scalar_prefetch=2,
            grid=(kv_heads, cached_steps + 1),
            in_specs=[q_spec] + pool_specs + [fresh_spec],
            out_specs=[o_spec, lse_spec],
            scratch_shapes=[
                pltpu.VMEM((rows, 1), jnp.float32),
                pltpu.VMEM((rows, 1), jnp.float32),
                pltpu.VMEM((rows, head_dim), jnp.float32),
            ],
        ),
        out_shape=[
            jax.ShapeDtypeStruct((kv_heads, rows, head_dim), jnp.bfloat16),
            jax.ShapeDtypeStruct((kv_heads, rows, 1), jnp.float32),
        ],
        compiler_params=pltpu.CompilerParams(dimension_semantics=("arbitrary", "arbitrary")),
        cost_estimate=cost,
    )(slots, meta, q_block, *([kv_pool] * pages_per_step), fresh)


def layer(tokens, norm_gain, w_query, w_key, w_value, w_out, kv_pool, cache_lengths, page_table):
    seq_position = lax.axis_index("seq")
    member = seq_position % GROUP
    group_id = seq_position // GROUP
    length = cache_lengths[group_id]
    first_new = length // PAGE
    table_row = page_table[group_id]
    tok_count = tokens.shape[0]
    kv_heads = w_key.shape[1] // HD
    q_heads = w_query.shape[1] // HD
    group_size = q_heads // kv_heads
    tok_pages = tok_count // PAGE
    cached_per_member = MAXLEN // PAGE // GROUP
    cached_steps = cached_per_member // PAGES_PER_STEP

    tp_size = lax.axis_size("tp")
    tp_index = lax.axis_index("tp")
    pieces = jnp.stack([tokens] + [tp_shift(tokens, s) for s in range(1, tp_size)])
    order = (tp_index - jnp.arange(tp_size, dtype=jnp.int32)) % tp_size
    whole = jnp.take(pieces, order, axis=0).transpose(1, 0, 2).reshape(tok_count, -1)
    rows_float = whole.astype(jnp.float32)
    normed = (
        rows_float
        * lax.rsqrt(jnp.mean(rows_float * rows_float, axis=-1, keepdims=True) + norm_eps)
        * norm_gain.astype(jnp.float32)
    ).astype(jnp.bfloat16)
    positions = length + member * tok_count + jnp.arange(tok_count, dtype=jnp.int32)
    query_rows = jnp.dot(normed, w_query, preferred_element_type=jnp.float32).reshape(
        tok_count, q_heads, HD
    )
    query = (
        rotate(query_rows, positions)
        .astype(jnp.bfloat16)
        .reshape(tok_count, kv_heads, group_size, HD)
    )
    key_rows = jnp.dot(normed, w_key, preferred_element_type=jnp.float32).reshape(
        tok_count, kv_heads, HD
    )
    new_keys = rotate(key_rows, positions).astype(jnp.bfloat16)
    new_values = (
        jnp.dot(normed, w_value, preferred_element_type=jnp.float32)
        .astype(jnp.bfloat16)
        .reshape(tok_count, kv_heads, HD)
    )
    key_pages = new_keys.reshape(tok_pages, PAGE, kv_heads, HD).transpose(0, 2, 3, 1)
    value_pages = new_values.reshape(tok_pages, PAGE, kv_heads, HD).transpose(0, 2, 3, 1)
    fresh_local = jnp.stack([key_pages, value_pages], axis=1)

    q_own = query.transpose(1, 0, 2, 3).reshape(kv_heads, tok_count * group_size, HD)
    q_blocks = [q_own]
    for s in range(1, GROUP):
        q_blocks.append(group_shift(q_own, "seq", s))
    fresh_all = [fresh_local] + [group_shift(fresh_local, "seq", s) for s in range(1, GROUP)]

    slots = table_row[member + GROUP * jnp.arange(cached_per_member, dtype=jnp.int32)]
    cached_count = jnp.maximum((first_new - member + GROUP - 1) // GROUP, 0)
    o_list = [None] * GROUP
    lse_list = [None] * GROUP
    for b in BLOCK_ORDER:
        source = (member - b) % GROUP
        meta = jnp.stack([cached_count, member, source]).astype(jnp.int32)
        o_b, lse_b = partial_attention(q_blocks[b], kv_pool, fresh_local, slots, meta, cached_steps)
        if b:
            o_b = group_shift(o_b, "seq", GROUP - b)
            lse_b = group_shift(lse_b, "seq", GROUP - b)
        o_list[b] = o_b
        lse_list[b] = lse_b
    lse_top = lse_list[0]
    for x in lse_list[1:]:
        lse_top = jnp.maximum(lse_top, x)
    weights = [jnp.exp(x - lse_top) for x in lse_list]
    weight_total = weights[0]
    for w in weights[1:]:
        weight_total = weight_total + w
    combined = weights[0] * o_list[0].astype(jnp.float32)
    for w, o in zip(weights[1:], o_list[1:]):
        combined = combined + w * o.astype(jnp.float32)
    combined = combined / weight_total
    attended = (
        combined.reshape(kv_heads, tok_count, group_size, HD)
        .transpose(1, 0, 2, 3)
        .reshape(tok_count, q_heads * HD)
        .astype(jnp.bfloat16)
    )
    out_term = jnp.dot(attended, w_out, preferred_element_type=jnp.float32)
    out_blocks = out_term.astype(jnp.bfloat16).reshape(tok_count, tp_size, -1)
    summed = lax.dynamic_index_in_dim(out_blocks, tp_index, 1, keepdims=False).astype(jnp.float32)
    for s in range(1, tp_size):
        piece = lax.dynamic_index_in_dim(out_blocks, (tp_index + s) % tp_size, 1, keepdims=False)
        summed = summed + tp_shift(piece, s).astype(jnp.float32)
    hidden = (tokens.astype(jnp.float32) + summed).astype(jnp.bfloat16)

    fresh_stack = jnp.stack(fresh_all)
    start_offset = (member - first_new) % GROUP
    new_pool = kv_pool
    for extra in range(2):
        page_id = start_offset + GROUP * extra
        source = page_id // tok_pages
        shift_id = (member - source) % GROUP
        page_piece = fresh_stack[shift_id, page_id % tok_pages]
        slot_id = table_row[first_new + page_id]
        new_pool = lax.dynamic_update_slice_in_dim(new_pool, page_piece[None], slot_id, 0)
    return (hidden, new_pool)


def solution(mesh):
    return jax.shard_map(
        layer,
        mesh=mesh,
        in_specs=(
            P("seq", "tp"),
            P(),
            P(None, "tp"),
            P(None, "tp"),
            P(None, "tp"),
            P("tp", None),
            P("seq", None, "tp", None, None),
            P(),
            P(),
        ),
        out_specs=(P("seq", "tp"), P("seq", None, "tp", None, None)),
        check_vma=False,
    )
```

```python
import functools

import jax
import jax.numpy as jnp
from jax import lax
from jax.experimental import pallas as pl
from jax.experimental.pallas import tpu as pltpu
from jax.sharding import PartitionSpec as P


HD = 80
PAGE = 128
MAXLEN = 8192
GROUP = 4
PAGES_PER_STEP = 8
BLOCK_ORDER = (0, 2, 1, 3)


norm_eps = 1e-05
rope_base = 1000000.0
masked_score = -1e30


def rotate(values, positions):
    head_dim = values.shape[-1]
    half_dim = head_dim // 2
    frequency = rope_base ** (-(jnp.arange(half_dim, dtype=jnp.float32) * 2.0) / head_dim)
    angles = positions.astype(jnp.float32)[:, None] * frequency[None, :]
    cosine = jnp.cos(angles)[:, None, :]
    sine_part = jnp.sin(angles)[:, None, :]
    first_half = values[..., :half_dim]
    second_half = values[..., half_dim:]
    return jnp.concatenate(
        [
            first_half * cosine - second_half * sine_part,
            second_half * cosine + first_half * sine_part,
        ],
        axis=-1,
    )


def group_shift(x, axis, shift):
    size = lax.axis_size(axis)
    pairs = [(i, i - i % GROUP + (i % GROUP + shift) % GROUP) for i in range(size)]
    return lax.ppermute(x, axis, pairs)


def tp_shift(x, shift):
    size = lax.axis_size("tp")
    return lax.ppermute(x, "tp", [(i, (i + shift) % size) for i in range(size)])


def partial_kernel(
    slots_ref, meta_ref, q_ref, *rest, pages_per_step, cached_steps, rows_per_tok, tok_count, scale
):
    pool_refs = rest[:pages_per_step]
    fresh_ref = rest[pages_per_step]
    o_ref, lse_ref = rest[pages_per_step + 1 : pages_per_step + 3]
    m_sc, l_sc, acc_sc = rest[pages_per_step + 3 :]
    step = pl.program_id(1)
    cached_count = meta_ref[0]
    member = meta_ref[1]
    source = meta_ref[2]

    @pl.when(step == 0)
    def _():
        m_sc[...] = jnp.full(m_sc.shape, masked_score, jnp.float32)
        l_sc[...] = jnp.zeros(l_sc.shape, jnp.float32)
        acc_sc[...] = jnp.zeros(acc_sc.shape, jnp.float32)

    def update(kv_pairs, page_flags, masks):
        q = q_ref[...]
        scores = []
        tops = []
        for (k, _), flag, mask in zip(kv_pairs, page_flags, masks):
            s = lax.dot_general(q, k, (((1,), (0,)), ((), ())), preferred_element_type=jnp.float32)
            if mask is not None:
                s = jnp.where(mask, s, masked_score)
            top = jnp.max(s, axis=1, keepdims=True)
            if flag is not None:
                top = jnp.where(flag, top, masked_score)
            scores.append(s)
            tops.append(top)
        m_prev = m_sc[...]
        m_new = m_prev
        for top in tops:
            m_new = jnp.maximum(m_new, top)
        alpha = jnp.exp((m_prev - m_new) * scale)
        l_new = alpha * l_sc[...]
        acc = alpha * acc_sc[...]
        for s, (_, v), flag, mask in zip(scores, kv_pairs, page_flags, masks):
            p = jnp.exp((s - m_new) * scale)
            if mask is not None:
                p = jnp.where(mask, p, 0.0)
            row_sum = jnp.sum(p, axis=1, keepdims=True)
            term = lax.dot_general(
                p.astype(jnp.bfloat16), v, (((1,), (1,)), ((), ())), preferred_element_type=jnp.float32
            )
            if flag is not None:
                row_sum = jnp.where(flag, row_sum, 0.0)
                term = jnp.where(flag, term, 0.0)
            l_new = l_new + row_sum
            acc = acc + term
        m_sc[...] = m_new
        l_sc[...] = l_new
        acc_sc[...] = acc

    cached_pairs = [(ref[0], ref[1]) for ref in pool_refs]
    first_page = step * pages_per_step

    @pl.when((step < cached_steps) & (first_page < cached_count))
    def _():
        flags = [first_page + i < cached_count for i in range(pages_per_step)]
        update(cached_pairs, flags, [None] * pages_per_step)

    fresh_pages = fresh_ref.shape[0]
    fresh_pairs = [(fresh_ref[e, 0], fresh_ref[e, 1]) for e in range(fresh_pages)]
    is_fresh = step == cached_steps

    @pl.when(is_fresh & (source >= member))
    def _():
        rows = q_ref.shape[0]
        row_tok = lax.broadcasted_iota(jnp.int32, (rows, PAGE), 0) // rows_per_tok
        col = lax.broadcasted_iota(jnp.int32, (rows, PAGE), 1)
        offset = (source - member) * tok_count
        masks = [e * PAGE + col <= row_tok + offset for e in range(fresh_pages)]
        update(fresh_pairs, [None] * fresh_pages, masks)

    @pl.when(is_fresh)
    def _():
        total = l_sc[...]
        filled = total > 0.0
        safe = jnp.where(filled, total, 1.0)
        o_ref[...] = (acc_sc[...] / safe).astype(o_ref.dtype)
        lse_ref[...] = jnp.where(filled, m_sc[...] * scale + jnp.log(safe), masked_score)


def partial_attention(q_block, kv_pool, fresh, slots, meta, cached_steps):
    kv_heads, rows, head_dim = q_block.shape
    pages_per_step = PAGES_PER_STEP
    fresh_pages = fresh.shape[0]
    tok_count = fresh_pages * PAGE
    rows_per_tok = rows // tok_count
    scale = head_dim ** (-0.5)

    def pool_map(i):
        def index_map(h, j, slots_ref, meta_ref):
            jj = jnp.minimum(j, cached_steps - 1)
            idx = jnp.minimum(jj * pages_per_step + i, jnp.maximum(meta_ref[0] - 1, 0))
            return (slots_ref[idx], 0, h, 0, 0)

        return index_map

    q_spec = pl.BlockSpec((None, rows, head_dim), lambda h, j, s, m: (h, 0, 0))
    pool_specs = [
        pl.BlockSpec((None, 2, None, head_dim, PAGE), pool_map(i)) for i in range(pages_per_step)
    ]
    fresh_spec = pl.BlockSpec(
        (fresh_pages, 2, None, head_dim, PAGE), lambda h, j, s, m: (0, 0, h, 0, 0)
    )
    o_spec = pl.BlockSpec((None, rows, head_dim), lambda h, j, s, m: (h, 0, 0))
    lse_spec = pl.BlockSpec((None, rows, 1), lambda h, j, s, m: (h, 0, 0))
    kernel = functools.partial(
        partial_kernel,
        pages_per_step=pages_per_step,
        cached_steps=cached_steps,
        rows_per_tok=rows_per_tok,
        tok_count=tok_count,
        scale=scale,
    )
    keys_per_row = cached_steps * pages_per_step * PAGE + tok_count
    cost = pl.CostEstimate(
        flops=4 * kv_heads * rows * keys_per_row * head_dim,
        transcendentals=kv_heads * rows * keys_per_row,
        bytes_accessed=2 * q_block.size * 3 + kv_heads * keys_per_row * head_dim * 4,
    )
    return pl.pallas_call(
        kernel,
        grid_spec=pltpu.PrefetchScalarGridSpec(
            num_scalar_prefetch=2,
            grid=(kv_heads, cached_steps + 1),
            in_specs=[q_spec] + pool_specs + [fresh_spec],
            out_specs=[o_spec, lse_spec],
            scratch_shapes=[
                pltpu.VMEM((rows, 1), jnp.float32),
                pltpu.VMEM((rows, 1), jnp.float32),
                pltpu.VMEM((rows, head_dim), jnp.float32),
            ],
        ),
        out_shape=[
            jax.ShapeDtypeStruct((kv_heads, rows, head_dim), jnp.bfloat16),
            jax.ShapeDtypeStruct((kv_heads, rows, 1), jnp.float32),
        ],
        compiler_params=pltpu.CompilerParams(dimension_semantics=("arbitrary", "arbitrary")),
        cost_estimate=cost,
    )(slots, meta, q_block, *([kv_pool] * pages_per_step), fresh)


def layer(tokens, norm_gain, w_query, w_key, w_value, w_out, kv_pool, cache_lengths, page_table):
    seq_position = lax.axis_index("seq")
    member = seq_position % GROUP
    group_id = seq_position // GROUP
    length = cache_lengths[group_id]
    first_new = length // PAGE
    table_row = page_table[group_id]
    tok_count = tokens.shape[0]
    kv_heads = w_key.shape[1] // HD
    q_heads = w_query.shape[1] // HD
    group_size = q_heads // kv_heads
    tok_pages = tok_count // PAGE
    cached_per_member = MAXLEN // PAGE // GROUP
    cached_steps = cached_per_member // PAGES_PER_STEP

    tp_size = lax.axis_size("tp")
    tp_index = lax.axis_index("tp")
    width = tokens.shape[1]
    whole = jnp.zeros((tok_count, width * tp_size), tokens.dtype)
    for s in range(tp_size):
        piece = tp_shift(tokens, s) if s else tokens
        column = (tp_index - s) % tp_size * width
        whole = lax.dynamic_update_slice(whole, piece, (0, column))
    rows_float = whole.astype(jnp.float32)
    normed = (
        rows_float
        * lax.rsqrt(jnp.mean(rows_float * rows_float, axis=-1, keepdims=True) + norm_eps)
        * norm_gain.astype(jnp.float32)
    ).astype(jnp.bfloat16)
    positions = length + member * tok_count + jnp.arange(tok_count, dtype=jnp.int32)
    query_rows = jnp.dot(normed, w_query, preferred_element_type=jnp.float32).reshape(
        tok_count, q_heads, HD
    )
    query = (
        rotate(query_rows, positions)
        .astype(jnp.bfloat16)
        .reshape(tok_count, kv_heads, group_size, HD)
    )
    key_rows = jnp.dot(normed, w_key, preferred_element_type=jnp.float32).reshape(
        tok_count, kv_heads, HD
    )
    new_keys = rotate(key_rows, positions).astype(jnp.bfloat16)
    new_values = (
        jnp.dot(normed, w_value, preferred_element_type=jnp.float32)
        .astype(jnp.bfloat16)
        .reshape(tok_count, kv_heads, HD)
    )
    key_pages = new_keys.reshape(tok_pages, PAGE, kv_heads, HD).transpose(0, 2, 3, 1)
    value_pages = new_values.reshape(tok_pages, PAGE, kv_heads, HD).transpose(0, 2, 3, 1)
    fresh_local = jnp.stack([key_pages, value_pages], axis=1)

    q_own = query.transpose(1, 0, 2, 3).reshape(kv_heads, tok_count * group_size, HD)
    q_blocks = [q_own]
    for s in range(1, GROUP):
        q_blocks.append(group_shift(q_own, "seq", s))
    fresh_all = [fresh_local] + [group_shift(fresh_local, "seq", s) for s in range(1, GROUP)]

    slots = table_row[member + GROUP * jnp.arange(cached_per_member, dtype=jnp.int32)]
    cached_count = jnp.maximum((first_new - member + GROUP - 1) // GROUP, 0)
    o_list = [None] * GROUP
    lse_list = [None] * GROUP
    for b in BLOCK_ORDER:
        source = (member - b) % GROUP
        meta = jnp.stack([cached_count, member, source]).astype(jnp.int32)
        o_b, lse_b = partial_attention(q_blocks[b], kv_pool, fresh_local, slots, meta, cached_steps)
        if b:
            o_b = group_shift(o_b, "seq", GROUP - b)
            lse_b = group_shift(lse_b, "seq", GROUP - b)
        o_list[b] = o_b
        lse_list[b] = lse_b
    lse_top = lse_list[0]
    for x in lse_list[1:]:
        lse_top = jnp.maximum(lse_top, x)
    weights = [jnp.exp(x - lse_top) for x in lse_list]
    weight_total = weights[0]
    for w in weights[1:]:
        weight_total = weight_total + w
    combined = weights[0] * o_list[0].astype(jnp.float32)
    for w, o in zip(weights[1:], o_list[1:]):
        combined = combined + w * o.astype(jnp.float32)
    combined = combined / weight_total
    attended = (
        combined.reshape(kv_heads, tok_count, group_size, HD)
        .transpose(1, 0, 2, 3)
        .reshape(tok_count, q_heads * HD)
        .astype(jnp.bfloat16)
    )
    out_blocks = jnp.einsum(
        "tk,kcn->ctn",
        attended,
        w_out.reshape(w_out.shape[0], tp_size, -1),
        preferred_element_type=jnp.float32,
    ).astype(jnp.bfloat16)
    summed = lax.dynamic_index_in_dim(out_blocks, tp_index, 0, keepdims=False).astype(jnp.float32)
    for s in range(1, tp_size):
        piece = lax.dynamic_index_in_dim(out_blocks, (tp_index + s) % tp_size, 0, keepdims=False)
        summed = summed + tp_shift(piece, s).astype(jnp.float32)
    hidden = (tokens.astype(jnp.float32) + summed).astype(jnp.bfloat16)

    fresh_stack = jnp.stack(fresh_all)
    start_offset = (member - first_new) % GROUP
    new_pool = kv_pool
    for extra in range(2):
        page_id = start_offset + GROUP * extra
        source = page_id // tok_pages
        shift_id = (member - source) % GROUP
        page_piece = fresh_stack[shift_id, page_id % tok_pages]
        slot_id = table_row[first_new + page_id]
        new_pool = lax.dynamic_update_slice_in_dim(new_pool, page_piece[None], slot_id, 0)
    return (hidden, new_pool)


def solution(mesh):
    return jax.shard_map(
        layer,
        mesh=mesh,
        in_specs=(
            P("seq", "tp"),
            P(),
            P(None, "tp"),
            P(None, "tp"),
            P(None, "tp"),
            P("tp", None),
            P("seq", None, "tp", None, None),
            P(),
            P(),
        ),
        out_specs=(P("seq", "tp"), P("seq", None, "tp", None, None)),
        check_vma=False,
    )
```

```python
import functools

import jax
import jax.numpy as jnp
from jax import lax
from jax.experimental import pallas as pl
from jax.experimental.pallas import tpu as pltpu
from jax.sharding import PartitionSpec as P


HD = 80
PAGE = 128
MAXLEN = 8192
GROUP = 4
PAGES_PER_STEP = 8


norm_eps = 1e-05
rope_base = 1000000.0
masked_score = -1e30


def rotate(values, positions):
    head_dim = values.shape[-1]
    half_dim = head_dim // 2
    frequency = rope_base ** (-(jnp.arange(half_dim, dtype=jnp.float32) * 2.0) / head_dim)
    angles = positions.astype(jnp.float32)[:, None] * frequency[None, :]
    cosine = jnp.cos(angles)[:, None, :]
    sine_part = jnp.sin(angles)[:, None, :]
    first_half = values[..., :half_dim]
    second_half = values[..., half_dim:]
    return jnp.concatenate(
        [
            first_half * cosine - second_half * sine_part,
            second_half * cosine + first_half * sine_part,
        ],
        axis=-1,
    )


def group_shift(x, axis, shift):
    size = lax.axis_size(axis)
    pairs = [(i, i - i % GROUP + (i % GROUP + shift) % GROUP) for i in range(size)]
    return lax.ppermute(x, axis, pairs)


def tp_shift(x, shift):
    size = lax.axis_size("tp")
    return lax.ppermute(x, "tp", [(i, (i + shift) % size) for i in range(size)])


def partial_kernel(
    slots_ref, meta_ref, q_ref, *rest, pages_per_step, cached_steps, rows_per_tok, tok_count, scale
):
    pool_refs = rest[:pages_per_step]
    fresh_ref = rest[pages_per_step]
    o_ref, lse_ref = rest[pages_per_step + 1 : pages_per_step + 3]
    m_sc, l_sc, acc_sc = rest[pages_per_step + 3 :]
    step = pl.program_id(1)
    cached_count = meta_ref[0]
    member = meta_ref[1]
    source = meta_ref[2]

    @pl.when(step == 0)
    def _():
        m_sc[...] = jnp.full(m_sc.shape, masked_score, jnp.float32)
        l_sc[...] = jnp.zeros(l_sc.shape, jnp.float32)
        acc_sc[...] = jnp.zeros(acc_sc.shape, jnp.float32)

    def update(kv_pairs, page_flags, masks):
        q = q_ref[...]
        scores = []
        tops = []
        for (k, _), flag, mask in zip(kv_pairs, page_flags, masks):
            s = lax.dot_general(q, k, (((1,), (0,)), ((), ())), preferred_element_type=jnp.float32)
            if mask is not None:
                s = jnp.where(mask, s, masked_score)
            top = jnp.max(s, axis=1, keepdims=True)
            if flag is not None:
                top = jnp.where(flag, top, masked_score)
            scores.append(s)
            tops.append(top)
        m_prev = m_sc[...]
        m_new = m_prev
        for top in tops:
            m_new = jnp.maximum(m_new, top)
        alpha = jnp.exp((m_prev - m_new) * scale)
        l_new = alpha * l_sc[...]
        acc = alpha * acc_sc[...]
        for s, (_, v), flag, mask in zip(scores, kv_pairs, page_flags, masks):
            p = jnp.exp((s - m_new) * scale)
            if mask is not None:
                p = jnp.where(mask, p, 0.0)
            row_sum = jnp.sum(p, axis=1, keepdims=True)
            term = lax.dot_general(
                p.astype(jnp.bfloat16), v, (((1,), (1,)), ((), ())), preferred_element_type=jnp.float32
            )
            if flag is not None:
                row_sum = jnp.where(flag, row_sum, 0.0)
                term = jnp.where(flag, term, 0.0)
            l_new = l_new + row_sum
            acc = acc + term
        m_sc[...] = m_new
        l_sc[...] = l_new
        acc_sc[...] = acc

    cached_pairs = [(ref[0], ref[1]) for ref in pool_refs]
    first_page = step * pages_per_step

    @pl.when((step < cached_steps) & (first_page < cached_count))
    def _():
        flags = [first_page + i < cached_count for i in range(pages_per_step)]
        update(cached_pairs, flags, [None] * pages_per_step)

    fresh_pages = fresh_ref.shape[0]
    fresh_pairs = [(fresh_ref[e, 0], fresh_ref[e, 1]) for e in range(fresh_pages)]
    is_fresh = step == cached_steps

    @pl.when(is_fresh & (source >= member))
    def _():
        rows = q_ref.shape[0]
        row_tok = lax.broadcasted_iota(jnp.int32, (rows, PAGE), 0) // rows_per_tok
        col = lax.broadcasted_iota(jnp.int32, (rows, PAGE), 1)
        offset = (source - member) * tok_count
        masks = [e * PAGE + col <= row_tok + offset for e in range(fresh_pages)]
        update(fresh_pairs, [None] * fresh_pages, masks)

    @pl.when(is_fresh)
    def _():
        total = l_sc[...]
        filled = total > 0.0
        safe = jnp.where(filled, total, 1.0)
        o_ref[...] = (acc_sc[...] / safe).astype(o_ref.dtype)
        lse_ref[...] = jnp.where(filled, m_sc[...] * scale + jnp.log(safe), masked_score)


def partial_attention(q_block, kv_pool, fresh, slots, meta, cached_steps, head0, kv_heads):
    _, rows, head_dim = q_block.shape
    pages_per_step = PAGES_PER_STEP
    fresh_pages = fresh.shape[0]
    tok_count = fresh_pages * PAGE
    rows_per_tok = rows // tok_count
    scale = head_dim ** (-0.5)

    def pool_map(i):
        def index_map(h, j, slots_ref, meta_ref):
            jj = jnp.minimum(j, cached_steps - 1)
            idx = jnp.minimum(jj * pages_per_step + i, jnp.maximum(meta_ref[0] - 1, 0))
            return (slots_ref[idx], 0, h + head0, 0, 0)

        return index_map

    q_spec = pl.BlockSpec((None, rows, head_dim), lambda h, j, s, m: (h + head0, 0, 0))
    pool_specs = [
        pl.BlockSpec((None, 2, None, head_dim, PAGE), pool_map(i)) for i in range(pages_per_step)
    ]
    fresh_spec = pl.BlockSpec(
        (fresh_pages, 2, None, head_dim, PAGE), lambda h, j, s, m: (0, 0, h + head0, 0, 0)
    )
    o_spec = pl.BlockSpec((None, rows, head_dim), lambda h, j, s, m: (h, 0, 0))
    lse_spec = pl.BlockSpec((None, rows, 1), lambda h, j, s, m: (h, 0, 0))
    kernel = functools.partial(
        partial_kernel,
        pages_per_step=pages_per_step,
        cached_steps=cached_steps,
        rows_per_tok=rows_per_tok,
        tok_count=tok_count,
        scale=scale,
    )
    keys_per_row = cached_steps * pages_per_step * PAGE + tok_count
    cost = pl.CostEstimate(
        flops=4 * kv_heads * rows * keys_per_row * head_dim,
        transcendentals=kv_heads * rows * keys_per_row,
        bytes_accessed=kv_heads * (rows * head_dim * 6 + keys_per_row * head_dim * 4),
    )
    return pl.pallas_call(
        kernel,
        grid_spec=pltpu.PrefetchScalarGridSpec(
            num_scalar_prefetch=2,
            grid=(kv_heads, cached_steps + 1),
            in_specs=[q_spec] + pool_specs + [fresh_spec],
            out_specs=[o_spec, lse_spec],
            scratch_shapes=[
                pltpu.VMEM((rows, 1), jnp.float32),
                pltpu.VMEM((rows, 1), jnp.float32),
                pltpu.VMEM((rows, head_dim), jnp.float32),
            ],
        ),
        out_shape=[
            jax.ShapeDtypeStruct((kv_heads, rows, head_dim), jnp.bfloat16),
            jax.ShapeDtypeStruct((kv_heads, rows, 1), jnp.float32),
        ],
        compiler_params=pltpu.CompilerParams(dimension_semantics=("arbitrary", "arbitrary")),
        cost_estimate=cost,
    )(slots, meta, q_block, *([kv_pool] * pages_per_step), fresh)


def layer(tokens, norm_gain, w_query, w_key, w_value, w_out, kv_pool, cache_lengths, page_table):
    seq_position = lax.axis_index("seq")
    member = seq_position % GROUP
    group_id = seq_position // GROUP
    length = cache_lengths[group_id]
    first_new = length // PAGE
    table_row = page_table[group_id]
    tok_count = tokens.shape[0]
    kv_heads = w_key.shape[1] // HD
    q_heads = w_query.shape[1] // HD
    group_size = q_heads // kv_heads
    tok_pages = tok_count // PAGE
    cached_per_member = MAXLEN // PAGE // GROUP
    cached_steps = cached_per_member // PAGES_PER_STEP

    tp_size = lax.axis_size("tp")
    tp_index = lax.axis_index("tp")
    width = tokens.shape[1]
    whole = jnp.zeros((tok_count, width * tp_size), tokens.dtype)
    for s in range(tp_size):
        piece = tp_shift(tokens, s) if s else tokens
        column = (tp_index - s) % tp_size * width
        whole = lax.dynamic_update_slice(whole, piece, (0, column))
    rows_float = whole.astype(jnp.float32)
    normed = (
        rows_float
        * lax.rsqrt(jnp.mean(rows_float * rows_float, axis=-1, keepdims=True) + norm_eps)
        * norm_gain.astype(jnp.float32)
    ).astype(jnp.bfloat16)
    positions = length + member * tok_count + jnp.arange(tok_count, dtype=jnp.int32)
    query_rows = jnp.dot(normed, w_query, preferred_element_type=jnp.float32).reshape(
        tok_count, q_heads, HD
    )
    query = (
        rotate(query_rows, positions)
        .astype(jnp.bfloat16)
        .reshape(tok_count, kv_heads, group_size, HD)
    )
    key_rows = jnp.dot(normed, w_key, preferred_element_type=jnp.float32).reshape(
        tok_count, kv_heads, HD
    )
    new_keys = rotate(key_rows, positions).astype(jnp.bfloat16)
    new_values = (
        jnp.dot(normed, w_value, preferred_element_type=jnp.float32)
        .astype(jnp.bfloat16)
        .reshape(tok_count, kv_heads, HD)
    )
    key_pages = new_keys.reshape(tok_pages, PAGE, kv_heads, HD).transpose(0, 2, 3, 1)
    value_pages = new_values.reshape(tok_pages, PAGE, kv_heads, HD).transpose(0, 2, 3, 1)
    fresh_local = jnp.stack([key_pages, value_pages], axis=1)

    q_own = query.transpose(1, 0, 2, 3).reshape(kv_heads, tok_count * group_size, HD)
    q_blocks = [q_own]
    for s in range(1, GROUP):
        q_blocks.append(group_shift(q_own, "seq", s))
    fresh_all = [fresh_local]
    for s in range(1, GROUP):
        fresh_all.append(group_shift(fresh_local, "seq", s))

    slots = table_row[member + GROUP * jnp.arange(cached_per_member, dtype=jnp.int32)]
    cached_count = jnp.maximum((first_new - member + GROUP - 1) // GROUP, 0)
    o_list = [None] * GROUP
    lse_list = [None] * GROUP
    own_o, own_lse = [], []
    for b, head0, n_heads in call_plan(kv_heads):
        source = (member - b) % GROUP
        meta = jnp.stack([cached_count, member, source]).astype(jnp.int32)
        o_b, lse_b = partial_attention(
            q_blocks[b], kv_pool, fresh_local, slots, meta, cached_steps, head0, n_heads
        )
        if b:
            o_list[b] = group_shift(o_b, "seq", GROUP - b)
            lse_list[b] = group_shift(lse_b, "seq", GROUP - b)
        else:
            own_o.append(o_b)
            own_lse.append(lse_b)
    o_list[0] = jnp.concatenate(own_o, axis=0)
    lse_list[0] = jnp.concatenate(own_lse, axis=0)
    lse_top = lse_list[0]
    for x in lse_list[1:]:
        lse_top = jnp.maximum(lse_top, x)
    weights = [jnp.exp(x - lse_top) for x in lse_list]
    weight_total = weights[0]
    for w in weights[1:]:
        weight_total = weight_total + w
    combined = weights[0] * o_list[0].astype(jnp.float32)
    for w, o in zip(weights[1:], o_list[1:]):
        combined = combined + w * o.astype(jnp.float32)
    combined = combined / weight_total
    attended = (
        combined.reshape(kv_heads, tok_count, group_size, HD)
        .transpose(1, 0, 2, 3)
        .reshape(tok_count, q_heads * HD)
        .astype(jnp.bfloat16)
    )
    out_blocks = jnp.einsum(
        "tk,kcn->ctn",
        attended,
        w_out.reshape(w_out.shape[0], tp_size, -1),
        preferred_element_type=jnp.float32,
    ).astype(jnp.bfloat16)
    summed = lax.dynamic_index_in_dim(out_blocks, tp_index, 0, keepdims=False).astype(jnp.float32)
    for s in range(1, tp_size):
        piece = lax.dynamic_index_in_dim(out_blocks, (tp_index + s) % tp_size, 0, keepdims=False)
        summed = summed + tp_shift(piece, s).astype(jnp.float32)
    hidden = (tokens.astype(jnp.float32) + summed).astype(jnp.bfloat16)

    fresh_stack = jnp.stack(fresh_all)
    start_offset = (member - first_new) % GROUP
    new_pool = kv_pool
    for extra in range(2):
        page_id = start_offset + GROUP * extra
        source = page_id // tok_pages
        shift_id = (member - source) % GROUP
        page_piece = fresh_stack[shift_id, page_id % tok_pages]
        slot_id = table_row[first_new + page_id]
        new_pool = lax.dynamic_update_slice_in_dim(new_pool, page_piece[None], slot_id, 0)
    return (hidden, new_pool)


def call_plan(kv_heads):
    half = kv_heads // 2
    plan = [(0, 0, half)]
    plan += [(b, 0, kv_heads) for b in range(1, GROUP)]
    plan += [(0, half, kv_heads - half)]
    return plan


def solution(mesh):
    return jax.shard_map(
        layer,
        mesh=mesh,
        in_specs=(
            P("seq", "tp"),
            P(),
            P(None, "tp"),
            P(None, "tp"),
            P(None, "tp"),
            P("tp", None),
            P("seq", None, "tp", None, None),
            P(),
            P(),
        ),
        out_specs=(P("seq", "tp"), P("seq", None, "tp", None, None)),
        check_vma=False,
    )
```

```python
import functools

import jax
import jax.numpy as jnp
from jax import lax
from jax.experimental import pallas as pl
from jax.experimental.pallas import tpu as pltpu
from jax.sharding import PartitionSpec as P


HD = 80
PAGE = 128
MAXLEN = 8192
GROUP = 4
PAGES_PER_STEP = 8


norm_eps = 1e-05
rope_base = 1000000.0
masked_score = -1e30


def rotate(values, positions):
    head_dim = values.shape[-1]
    half_dim = head_dim // 2
    frequency = rope_base ** (-(jnp.arange(half_dim, dtype=jnp.float32) * 2.0) / head_dim)
    angles = positions.astype(jnp.float32)[:, None] * frequency[None, :]
    cosine = jnp.cos(angles)[:, None, :]
    sine_part = jnp.sin(angles)[:, None, :]
    first_half = values[..., :half_dim]
    second_half = values[..., half_dim:]
    return jnp.concatenate(
        [
            first_half * cosine - second_half * sine_part,
            second_half * cosine + first_half * sine_part,
        ],
        axis=-1,
    )


def group_shift(x, axis, shift):
    size = lax.axis_size(axis)
    pairs = [(i, i - i % GROUP + (i % GROUP + shift) % GROUP) for i in range(size)]
    return lax.ppermute(x, axis, pairs)


def tp_shift(x, shift):
    size = lax.axis_size("tp")
    return lax.ppermute(x, "tp", [(i, (i + shift) % size) for i in range(size)])


def partial_kernel(
    slots_ref, meta_ref, q_ref, *rest, pages_per_step, cached_steps, rows_per_tok, tok_count, scale
):
    pool_refs = rest[:pages_per_step]
    fresh_ref = rest[pages_per_step]
    o_ref, lse_ref = rest[pages_per_step + 1 : pages_per_step + 3]
    m_sc, l_sc, acc_sc = rest[pages_per_step + 3 :]
    step = pl.program_id(1)
    cached_count = meta_ref[0]
    member = meta_ref[1]
    source = meta_ref[2]

    @pl.when(step == 0)
    def _():
        m_sc[...] = jnp.full(m_sc.shape, masked_score, jnp.float32)
        l_sc[...] = jnp.zeros(l_sc.shape, jnp.float32)
        acc_sc[...] = jnp.zeros(acc_sc.shape, jnp.float32)

    def update(kv_pairs, page_flags, masks):
        q = q_ref[...]
        scores = []
        tops = []
        for (k, _), flag, mask in zip(kv_pairs, page_flags, masks):
            s = lax.dot_general(q, k, (((1,), (0,)), ((), ())), preferred_element_type=jnp.float32)
            if mask is not None:
                s = jnp.where(mask, s, masked_score)
            top = jnp.max(s, axis=1, keepdims=True)
            if flag is not None:
                top = jnp.where(flag, top, masked_score)
            scores.append(s)
            tops.append(top)
        m_prev = m_sc[...]
        m_new = m_prev
        for top in tops:
            m_new = jnp.maximum(m_new, top)
        alpha = jnp.exp((m_prev - m_new) * scale)
        l_new = alpha * l_sc[...]
        acc = alpha * acc_sc[...]
        for s, (_, v), flag, mask in zip(scores, kv_pairs, page_flags, masks):
            p = jnp.exp((s - m_new) * scale)
            if mask is not None:
                p = jnp.where(mask, p, 0.0)
            row_sum = jnp.sum(p, axis=1, keepdims=True)
            term = lax.dot_general(
                p.astype(jnp.bfloat16), v, (((1,), (1,)), ((), ())), preferred_element_type=jnp.float32
            )
            if flag is not None:
                row_sum = jnp.where(flag, row_sum, 0.0)
                term = jnp.where(flag, term, 0.0)
            l_new = l_new + row_sum
            acc = acc + term
        m_sc[...] = m_new
        l_sc[...] = l_new
        acc_sc[...] = acc

    cached_pairs = [(ref[0], ref[1]) for ref in pool_refs]
    first_page = step * pages_per_step

    @pl.when((step < cached_steps) & (first_page < cached_count))
    def _():
        flags = [first_page + i < cached_count for i in range(pages_per_step)]
        update(cached_pairs, flags, [None] * pages_per_step)

    fresh_pages = fresh_ref.shape[0]
    fresh_pairs = [(fresh_ref[e, 0], fresh_ref[e, 1]) for e in range(fresh_pages)]
    is_fresh = step == cached_steps

    @pl.when(is_fresh & (source >= member))
    def _():
        rows = q_ref.shape[0]
        row_tok = lax.broadcasted_iota(jnp.int32, (rows, PAGE), 0) // rows_per_tok
        col = lax.broadcasted_iota(jnp.int32, (rows, PAGE), 1)
        offset = (source - member) * tok_count
        masks = [e * PAGE + col <= row_tok + offset for e in range(fresh_pages)]
        update(fresh_pairs, [None] * fresh_pages, masks)

    @pl.when(is_fresh)
    def _():
        total = l_sc[...]
        filled = total > 0.0
        safe = jnp.where(filled, total, 1.0)
        o_ref[...] = (acc_sc[...] / safe).astype(o_ref.dtype)
        lse = jnp.where(filled, m_sc[...] * scale + jnp.log(safe), masked_score)
        wide = jnp.transpose(jnp.broadcast_to(lse, (lse.shape[0], 128)))
        lse_ref[...] = wide[0:1, :]


def partial_attention(q_block, kv_pool, fresh, slots, meta, cached_steps, head0, kv_heads, rows):
    head_dim = q_block.shape[2]
    pages_per_step = PAGES_PER_STEP
    fresh_pages = fresh.shape[0]
    tok_count = fresh_pages * PAGE
    rows_per_tok = rows // tok_count
    scale = head_dim ** (-0.5)

    def pool_map(i):
        def index_map(h, j, slots_ref, meta_ref):
            jj = jnp.minimum(j, cached_steps - 1)
            idx = jnp.minimum(jj * pages_per_step + i, jnp.maximum(meta_ref[0] - 1, 0))
            return (slots_ref[idx], 0, h + head0, 0, 0)

        return index_map

    q_spec = pl.BlockSpec((None, rows, head_dim), lambda h, j, s, m: (h + head0, 0, 0))
    pool_specs = [
        pl.BlockSpec((None, 2, None, head_dim, PAGE), pool_map(i)) for i in range(pages_per_step)
    ]
    fresh_spec = pl.BlockSpec(
        (fresh_pages, 2, None, head_dim, PAGE), lambda h, j, s, m: (0, 0, h + head0, 0, 0)
    )
    o_spec = pl.BlockSpec((None, rows, head_dim), lambda h, j, s, m: (h, 0, 0))
    lse_spec = pl.BlockSpec((None, 1, rows), lambda h, j, s, m: (h, 0, 0))
    kernel = functools.partial(
        partial_kernel,
        pages_per_step=pages_per_step,
        cached_steps=cached_steps,
        rows_per_tok=rows_per_tok,
        tok_count=tok_count,
        scale=scale,
    )
    keys_per_row = cached_steps * pages_per_step * PAGE + tok_count
    cost = pl.CostEstimate(
        flops=4 * kv_heads * rows * keys_per_row * head_dim,
        transcendentals=kv_heads * rows * keys_per_row,
        bytes_accessed=kv_heads * (rows * head_dim * 6 + keys_per_row * head_dim * 4),
    )
    return pl.pallas_call(
        kernel,
        grid_spec=pltpu.PrefetchScalarGridSpec(
            num_scalar_prefetch=2,
            grid=(kv_heads, cached_steps + 1),
            in_specs=[q_spec] + pool_specs + [fresh_spec],
            out_specs=[o_spec, lse_spec],
            scratch_shapes=[
                pltpu.VMEM((rows, 1), jnp.float32),
                pltpu.VMEM((rows, 1), jnp.float32),
                pltpu.VMEM((rows, head_dim), jnp.float32),
            ],
        ),
        out_shape=[
            jax.ShapeDtypeStruct((kv_heads, rows, head_dim), jnp.bfloat16),
            jax.ShapeDtypeStruct((kv_heads, 1, rows), jnp.float32),
        ],
        compiler_params=pltpu.CompilerParams(dimension_semantics=("arbitrary", "arbitrary")),
        cost_estimate=cost,
    )(slots, meta, q_block, *([kv_pool] * pages_per_step), fresh)


def layer(tokens, norm_gain, w_query, w_key, w_value, w_out, kv_pool, cache_lengths, page_table):
    seq_position = lax.axis_index("seq")
    member = seq_position % GROUP
    group_id = seq_position // GROUP
    length = cache_lengths[group_id]
    first_new = length // PAGE
    table_row = page_table[group_id]
    tok_count = tokens.shape[0]
    kv_heads = w_key.shape[1] // HD
    q_heads = w_query.shape[1] // HD
    group_size = q_heads // kv_heads
    tok_pages = tok_count // PAGE
    cached_per_member = MAXLEN // PAGE // GROUP
    cached_steps = cached_per_member // PAGES_PER_STEP

    tp_size = lax.axis_size("tp")
    tp_index = lax.axis_index("tp")
    width = tokens.shape[1]
    whole = jnp.zeros((tok_count, width * tp_size), tokens.dtype)
    for s in range(tp_size):
        piece = tp_shift(tokens, s) if s else tokens
        column = (tp_index - s) % tp_size * width
        whole = lax.dynamic_update_slice(whole, piece, (0, column))
    rows_float = whole.astype(jnp.float32)
    normed = (
        rows_float
        * lax.rsqrt(jnp.mean(rows_float * rows_float, axis=-1, keepdims=True) + norm_eps)
        * norm_gain.astype(jnp.float32)
    ).astype(jnp.bfloat16)
    positions = length + member * tok_count + jnp.arange(tok_count, dtype=jnp.int32)
    query_rows = jnp.dot(normed, w_query, preferred_element_type=jnp.float32).reshape(
        tok_count, q_heads, HD
    )
    query = (
        rotate(query_rows, positions)
        .astype(jnp.bfloat16)
        .reshape(tok_count, kv_heads, group_size, HD)
    )
    key_rows = jnp.dot(normed, w_key, preferred_element_type=jnp.float32).reshape(
        tok_count, kv_heads, HD
    )
    new_keys = rotate(key_rows, positions).astype(jnp.bfloat16)
    new_values = (
        jnp.dot(normed, w_value, preferred_element_type=jnp.float32)
        .astype(jnp.bfloat16)
        .reshape(tok_count, kv_heads, HD)
    )
    key_pages = new_keys.reshape(tok_pages, PAGE, kv_heads, HD).transpose(0, 2, 3, 1)
    value_pages = new_values.reshape(tok_pages, PAGE, kv_heads, HD).transpose(0, 2, 3, 1)
    fresh_local = jnp.stack([key_pages, value_pages], axis=1)

    q_own = query.transpose(1, 0, 2, 3).reshape(kv_heads, tok_count * group_size, HD)
    q_rows = q_own.shape[1]
    carried = jnp.concatenate([q_own, fresh_local.reshape(kv_heads, -1, HD)], axis=1)
    q_blocks = [q_own]
    fresh_all = [fresh_local]
    for s in range(1, GROUP):
        arrived = group_shift(carried, "seq", s)
        q_blocks.append(arrived)
        fresh_all.append(arrived[:, q_rows:].reshape(fresh_local.shape))

    slots = table_row[member + GROUP * jnp.arange(cached_per_member, dtype=jnp.int32)]
    cached_count = jnp.maximum((first_new - member + GROUP - 1) // GROUP, 0)
    o_list = [None] * GROUP
    lse_list = [None] * GROUP
    own_o, own_lse = [], []
    for b, head0, n_heads in call_plan(kv_heads):
        source = (member - b) % GROUP
        meta = jnp.stack([cached_count, member, source]).astype(jnp.int32)
        o_b, lse_b = partial_attention(
            q_blocks[b], kv_pool, fresh_local, slots, meta, cached_steps, head0, n_heads, q_rows
        )
        if b:
            o_list[b] = group_shift(o_b, "seq", GROUP - b)
            lse_list[b] = group_shift(lse_b, "seq", GROUP - b)
        else:
            own_o.append(o_b)
            own_lse.append(lse_b)
    o_list[0] = jnp.concatenate(own_o, axis=0)
    lse_list[0] = jnp.concatenate(own_lse, axis=0)
    lse_list = [x.reshape(kv_heads, -1, 1) for x in lse_list]
    lse_top = lse_list[0]
    for x in lse_list[1:]:
        lse_top = jnp.maximum(lse_top, x)
    weights = [jnp.exp(x - lse_top) for x in lse_list]
    weight_total = weights[0]
    for w in weights[1:]:
        weight_total = weight_total + w
    combined = weights[0] * o_list[0].astype(jnp.float32)
    for w, o in zip(weights[1:], o_list[1:]):
        combined = combined + w * o.astype(jnp.float32)
    combined = combined / weight_total
    attended = (
        combined.reshape(kv_heads, tok_count, group_size, HD)
        .transpose(1, 0, 2, 3)
        .reshape(tok_count, q_heads * HD)
        .astype(jnp.bfloat16)
    )
    out_blocks = jnp.einsum(
        "tk,kcn->ctn",
        attended,
        w_out.reshape(w_out.shape[0], tp_size, -1),
        preferred_element_type=jnp.float32,
    ).astype(jnp.bfloat16)
    summed = lax.dynamic_index_in_dim(out_blocks, tp_index, 0, keepdims=False).astype(jnp.float32)
    for s in range(1, tp_size):
        piece = lax.dynamic_index_in_dim(out_blocks, (tp_index + s) % tp_size, 0, keepdims=False)
        summed = summed + tp_shift(piece, s).astype(jnp.float32)
    hidden = (tokens.astype(jnp.float32) + summed).astype(jnp.bfloat16)

    fresh_stack = jnp.stack(fresh_all)
    start_offset = (member - first_new) % GROUP
    new_pool = kv_pool
    for extra in range(2):
        page_id = start_offset + GROUP * extra
        source = page_id // tok_pages
        shift_id = (member - source) % GROUP
        page_piece = fresh_stack[shift_id, page_id % tok_pages]
        slot_id = table_row[first_new + page_id]
        new_pool = lax.dynamic_update_slice_in_dim(new_pool, page_piece[None], slot_id, 0)
    return (hidden, new_pool)


def call_plan(kv_heads):
    half = kv_heads // 2
    plan = [(0, 0, half)]
    plan += [(b, 0, kv_heads) for b in range(1, GROUP)]
    plan += [(0, half, kv_heads - half)]
    return plan


def solution(mesh):
    return jax.shard_map(
        layer,
        mesh=mesh,
        in_specs=(
            P("seq", "tp"),
            P(),
            P(None, "tp"),
            P(None, "tp"),
            P(None, "tp"),
            P("tp", None),
            P("seq", None, "tp", None, None),
            P(),
            P(),
        ),
        out_specs=(P("seq", "tp"), P("seq", None, "tp", None, None)),
        check_vma=False,
    )
```

```python
import functools

import jax
import jax.numpy as jnp
from jax import lax
from jax.experimental import pallas as pl
from jax.experimental.pallas import tpu as pltpu
from jax.sharding import PartitionSpec as P


HD = 80
PAGE = 128
MAXLEN = 8192
GROUP = 4
PAGES_PER_STEP = 16


norm_eps = 1e-05
rope_base = 1000000.0
masked_score = -1e30


def rotate(values, positions):
    head_dim = values.shape[-1]
    half_dim = head_dim // 2
    frequency = rope_base ** (-(jnp.arange(half_dim, dtype=jnp.float32) * 2.0) / head_dim)
    angles = positions.astype(jnp.float32)[:, None] * frequency[None, :]
    cosine = jnp.cos(angles)[:, None, :]
    sine_part = jnp.sin(angles)[:, None, :]
    first_half = values[..., :half_dim]
    second_half = values[..., half_dim:]
    return jnp.concatenate(
        [
            first_half * cosine - second_half * sine_part,
            second_half * cosine + first_half * sine_part,
        ],
        axis=-1,
    )


def group_shift(x, axis, shift):
    size = lax.axis_size(axis)
    pairs = [(i, i - i % GROUP + (i % GROUP + shift) % GROUP) for i in range(size)]
    return lax.ppermute(x, axis, pairs)


def tp_shift(x, shift):
    size = lax.axis_size("tp")
    return lax.ppermute(x, "tp", [(i, (i + shift) % size) for i in range(size)])


def partial_kernel(
    slots_ref, meta_ref, q_ref, *rest, pages_per_step, cached_steps, rows_per_tok, tok_count, scale
):
    pool_refs = rest[:pages_per_step]
    fresh_ref = rest[pages_per_step]
    o_ref, lse_ref = rest[pages_per_step + 1 : pages_per_step + 3]
    m_sc, l_sc, acc_sc = rest[pages_per_step + 3 :]
    step = pl.program_id(1)
    cached_count = meta_ref[0]
    member = meta_ref[1]
    source = meta_ref[2]

    @pl.when(step == 0)
    def _():
        m_sc[...] = jnp.full(m_sc.shape, masked_score, jnp.float32)
        l_sc[...] = jnp.zeros(l_sc.shape, jnp.float32)
        acc_sc[...] = jnp.zeros(acc_sc.shape, jnp.float32)

    def update(kv_pairs, page_flags, masks):
        q = q_ref[...]
        scores = []
        tops = []
        for (k, _), flag, mask in zip(kv_pairs, page_flags, masks):
            s = lax.dot_general(q, k, (((1,), (0,)), ((), ())), preferred_element_type=jnp.float32)
            if mask is not None:
                s = jnp.where(mask, s, masked_score)
            top = jnp.max(s, axis=1, keepdims=True)
            if flag is not None:
                top = jnp.where(flag, top, masked_score)
            scores.append(s)
            tops.append(top)
        m_prev = m_sc[...]
        m_new = m_prev
        for top in tops:
            m_new = jnp.maximum(m_new, top)
        alpha = jnp.exp((m_prev - m_new) * scale)
        l_new = alpha * l_sc[...]
        acc = alpha * acc_sc[...]
        for s, (_, v), flag, mask in zip(scores, kv_pairs, page_flags, masks):
            p = jnp.exp((s - m_new) * scale)
            if mask is not None:
                p = jnp.where(mask, p, 0.0)
            row_sum = jnp.sum(p, axis=1, keepdims=True)
            term = lax.dot_general(
                p.astype(jnp.bfloat16), v, (((1,), (1,)), ((), ())), preferred_element_type=jnp.float32
            )
            if flag is not None:
                row_sum = jnp.where(flag, row_sum, 0.0)
                term = jnp.where(flag, term, 0.0)
            l_new = l_new + row_sum
            acc = acc + term
        m_sc[...] = m_new
        l_sc[...] = l_new
        acc_sc[...] = acc

    cached_pairs = [(ref[0], ref[1]) for ref in pool_refs]
    first_page = step * pages_per_step

    @pl.when((step < cached_steps) & (first_page < cached_count))
    def _():
        flags = [first_page + i < cached_count for i in range(pages_per_step)]
        update(cached_pairs, flags, [None] * pages_per_step)

    fresh_pages = fresh_ref.shape[0]
    fresh_pairs = [(fresh_ref[e, 0], fresh_ref[e, 1]) for e in range(fresh_pages)]
    is_fresh = step == cached_steps

    @pl.when(is_fresh & (source >= member))
    def _():
        rows = q_ref.shape[0]
        row_tok = lax.broadcasted_iota(jnp.int32, (rows, PAGE), 0) // rows_per_tok
        col = lax.broadcasted_iota(jnp.int32, (rows, PAGE), 1)
        offset = (source - member) * tok_count
        masks = [e * PAGE + col <= row_tok + offset for e in range(fresh_pages)]
        update(fresh_pairs, [None] * fresh_pages, masks)

    @pl.when(is_fresh)
    def _():
        total = l_sc[...]
        filled = total > 0.0
        safe = jnp.where(filled, total, 1.0)
        o_ref[...] = (acc_sc[...] / safe).astype(o_ref.dtype)
        lse = jnp.where(filled, m_sc[...] * scale + jnp.log(safe), masked_score)
        wide = jnp.transpose(jnp.broadcast_to(lse, (lse.shape[0], 128)))
        lse_ref[...] = wide[0:1, :]


def partial_attention(q_block, kv_pool, fresh, slots, meta, cached_steps, head0, kv_heads):
    _, rows, head_dim = q_block.shape
    pages_per_step = PAGES_PER_STEP
    fresh_pages = fresh.shape[0]
    tok_count = fresh_pages * PAGE
    rows_per_tok = rows // tok_count
    scale = head_dim ** (-0.5)

    def pool_map(i):
        def index_map(h, j, slots_ref, meta_ref):
            jj = jnp.minimum(j, cached_steps - 1)
            idx = jnp.minimum(jj * pages_per_step + i, jnp.maximum(meta_ref[0] - 1, 0))
            return (slots_ref[idx], 0, h + head0, 0, 0)

        return index_map

    q_spec = pl.BlockSpec((None, rows, head_dim), lambda h, j, s, m: (h + head0, 0, 0))
    pool_specs = [
        pl.BlockSpec((None, 2, None, head_dim, PAGE), pool_map(i)) for i in range(pages_per_step)
    ]
    fresh_spec = pl.BlockSpec(
        (fresh_pages, 2, None, head_dim, PAGE), lambda h, j, s, m: (0, 0, h + head0, 0, 0)
    )
    o_spec = pl.BlockSpec((None, rows, head_dim), lambda h, j, s, m: (h, 0, 0))
    lse_spec = pl.BlockSpec((None, 1, rows), lambda h, j, s, m: (h, 0, 0))
    kernel = functools.partial(
        partial_kernel,
        pages_per_step=pages_per_step,
        cached_steps=cached_steps,
        rows_per_tok=rows_per_tok,
        tok_count=tok_count,
        scale=scale,
    )
    keys_per_row = cached_steps * pages_per_step * PAGE + tok_count
    cost = pl.CostEstimate(
        flops=4 * kv_heads * rows * keys_per_row * head_dim,
        transcendentals=kv_heads * rows * keys_per_row,
        bytes_accessed=kv_heads * (rows * head_dim * 6 + keys_per_row * head_dim * 4),
    )
    return pl.pallas_call(
        kernel,
        grid_spec=pltpu.PrefetchScalarGridSpec(
            num_scalar_prefetch=2,
            grid=(kv_heads, cached_steps + 1),
            in_specs=[q_spec] + pool_specs + [fresh_spec],
            out_specs=[o_spec, lse_spec],
            scratch_shapes=[
                pltpu.VMEM((rows, 1), jnp.float32),
                pltpu.VMEM((rows, 1), jnp.float32),
                pltpu.VMEM((rows, head_dim), jnp.float32),
            ],
        ),
        out_shape=[
            jax.ShapeDtypeStruct((kv_heads, rows, head_dim), jnp.bfloat16),
            jax.ShapeDtypeStruct((kv_heads, 1, rows), jnp.float32),
        ],
        compiler_params=pltpu.CompilerParams(dimension_semantics=("arbitrary", "arbitrary")),
        cost_estimate=cost,
    )(slots, meta, q_block, *([kv_pool] * pages_per_step), fresh)


def layer(tokens, norm_gain, w_query, w_key, w_value, w_out, kv_pool, cache_lengths, page_table):
    seq_position = lax.axis_index("seq")
    member = seq_position % GROUP
    group_id = seq_position // GROUP
    length = cache_lengths[group_id]
    first_new = length // PAGE
    table_row = page_table[group_id]
    tok_count = tokens.shape[0]
    kv_heads = w_key.shape[1] // HD
    q_heads = w_query.shape[1] // HD
    group_size = q_heads // kv_heads
    tok_pages = tok_count // PAGE
    cached_per_member = MAXLEN // PAGE // GROUP
    cached_steps = cached_per_member // PAGES_PER_STEP

    tp_size = lax.axis_size("tp")
    tp_index = lax.axis_index("tp")
    width = tokens.shape[1]
    whole = jnp.zeros((tok_count, width * tp_size), tokens.dtype)
    for s in range(tp_size):
        piece = tp_shift(tokens, s) if s else tokens
        column = (tp_index - s) % tp_size * width
        whole = lax.dynamic_update_slice(whole, piece, (0, column))
    rows_float = whole.astype(jnp.float32)
    normed = (
        rows_float
        * lax.rsqrt(jnp.mean(rows_float * rows_float, axis=-1, keepdims=True) + norm_eps)
        * norm_gain.astype(jnp.float32)
    ).astype(jnp.bfloat16)
    positions = length + member * tok_count + jnp.arange(tok_count, dtype=jnp.int32)
    query_rows = jnp.dot(normed, w_query, preferred_element_type=jnp.float32).reshape(
        tok_count, q_heads, HD
    )
    query = (
        rotate(query_rows, positions)
        .astype(jnp.bfloat16)
        .reshape(tok_count, kv_heads, group_size, HD)
    )
    key_rows = jnp.dot(normed, w_key, preferred_element_type=jnp.float32).reshape(
        tok_count, kv_heads, HD
    )
    new_keys = rotate(key_rows, positions).astype(jnp.bfloat16)
    new_values = (
        jnp.dot(normed, w_value, preferred_element_type=jnp.float32)
        .astype(jnp.bfloat16)
        .reshape(tok_count, kv_heads, HD)
    )
    key_pages = new_keys.reshape(tok_pages, PAGE, kv_heads, HD).transpose(0, 2, 3, 1)
    value_pages = new_values.reshape(tok_pages, PAGE, kv_heads, HD).transpose(0, 2, 3, 1)
    fresh_local = jnp.stack([key_pages, value_pages], axis=1)

    q_own = query.transpose(1, 0, 2, 3).reshape(kv_heads, tok_count * group_size, HD)
    q_blocks = [q_own]
    for s in range(1, GROUP):
        q_blocks.append(group_shift(q_own, "seq", s))
    fresh_all = [fresh_local]
    for s in range(1, GROUP):
        fresh_all.append(group_shift(fresh_local, "seq", s))

    slots = table_row[member + GROUP * jnp.arange(cached_per_member, dtype=jnp.int32)]
    cached_count = jnp.maximum((first_new - member + GROUP - 1) // GROUP, 0)
    o_list = [None] * GROUP
    lse_list = [None] * GROUP
    own_o, own_lse = [], []
    for b, head0, n_heads in call_plan(kv_heads):
        source = (member - b) % GROUP
        meta = jnp.stack([cached_count, member, source]).astype(jnp.int32)
        o_b, lse_b = partial_attention(
            q_blocks[b], kv_pool, fresh_local, slots, meta, cached_steps, head0, n_heads
        )
        if b:
            o_list[b] = group_shift(o_b, "seq", GROUP - b)
            lse_list[b] = group_shift(lse_b, "seq", GROUP - b)
        else:
            own_o.append(o_b)
            own_lse.append(lse_b)
    o_list[0] = jnp.concatenate(own_o, axis=0)
    lse_list[0] = jnp.concatenate(own_lse, axis=0)
    lse_list = [x.reshape(kv_heads, -1, 1) for x in lse_list]
    lse_top = lse_list[0]
    for x in lse_list[1:]:
        lse_top = jnp.maximum(lse_top, x)
    weights = [jnp.exp(x - lse_top) for x in lse_list]
    weight_total = weights[0]
    for w in weights[1:]:
        weight_total = weight_total + w
    combined = weights[0] * o_list[0].astype(jnp.float32)
    for w, o in zip(weights[1:], o_list[1:]):
        combined = combined + w * o.astype(jnp.float32)
    combined = combined / weight_total
    attended = (
        combined.reshape(kv_heads, tok_count, group_size, HD)
        .transpose(1, 0, 2, 3)
        .reshape(tok_count, q_heads * HD)
        .astype(jnp.bfloat16)
    )
    out_blocks = jnp.einsum(
        "tk,kcn->ctn",
        attended,
        w_out.reshape(w_out.shape[0], tp_size, -1),
        preferred_element_type=jnp.float32,
    ).astype(jnp.bfloat16)
    summed = lax.dynamic_index_in_dim(out_blocks, tp_index, 0, keepdims=False).astype(jnp.float32)
    for s in range(1, tp_size):
        piece = lax.dynamic_index_in_dim(out_blocks, (tp_index + s) % tp_size, 0, keepdims=False)
        summed = summed + tp_shift(piece, s).astype(jnp.float32)
    hidden = (tokens.astype(jnp.float32) + summed).astype(jnp.bfloat16)

    fresh_stack = jnp.stack(fresh_all)
    start_offset = (member - first_new) % GROUP
    new_pool = kv_pool
    for extra in range(2):
        page_id = start_offset + GROUP * extra
        source = page_id // tok_pages
        shift_id = (member - source) % GROUP
        page_piece = fresh_stack[shift_id, page_id % tok_pages]
        slot_id = table_row[first_new + page_id]
        new_pool = lax.dynamic_update_slice_in_dim(new_pool, page_piece[None], slot_id, 0)
    return (hidden, new_pool)


def call_plan(kv_heads):
    half = kv_heads // 2
    plan = [(0, 0, half)]
    plan += [(b, 0, kv_heads) for b in range(1, GROUP)]
    plan += [(0, half, kv_heads - half)]
    return plan


def solution(mesh):
    return jax.shard_map(
        layer,
        mesh=mesh,
        in_specs=(
            P("seq", "tp"),
            P(),
            P(None, "tp"),
            P(None, "tp"),
            P(None, "tp"),
            P("tp", None),
            P("seq", None, "tp", None, None),
            P(),
            P(),
        ),
        out_specs=(P("seq", "tp"), P("seq", None, "tp", None, None)),
        check_vma=False,
    )
```

```python
import functools

import jax
import jax.numpy as jnp
from jax import lax
from jax.experimental import pallas as pl
from jax.experimental.pallas import tpu as pltpu
from jax.sharding import PartitionSpec as P


HD = 80
PAGE = 128
MAXLEN = 8192
GROUP = 4
PAGES_PER_STEP = 8


norm_eps = 1e-05
rope_base = 1000000.0
masked_score = -1e30


def rotate(values, positions):
    head_dim = values.shape[-1]
    half_dim = head_dim // 2
    frequency = rope_base ** (-(jnp.arange(half_dim, dtype=jnp.float32) * 2.0) / head_dim)
    angles = positions.astype(jnp.float32)[:, None] * frequency[None, :]
    cosine = jnp.cos(angles)[:, None, :]
    sine_part = jnp.sin(angles)[:, None, :]
    first_half = values[..., :half_dim]
    second_half = values[..., half_dim:]
    return jnp.concatenate(
        [
            first_half * cosine - second_half * sine_part,
            second_half * cosine + first_half * sine_part,
        ],
        axis=-1,
    )


def group_shift(x, axis, shift):
    size = lax.axis_size(axis)
    pairs = [(i, i - i % GROUP + (i % GROUP + shift) % GROUP) for i in range(size)]
    return lax.ppermute(x, axis, pairs)


def tp_swap(x, bit):
    size = lax.axis_size("tp")
    return lax.ppermute(x, "tp", [(i, i ^ bit) for i in range(size)])


def partial_kernel(
    slots_ref, meta_ref, q_ref, *rest, pages_per_step, cached_steps, rows_per_tok, tok_count, scale
):
    pool_refs = rest[:pages_per_step]
    fresh_ref = rest[pages_per_step]
    o_ref, lse_ref = rest[pages_per_step + 1 : pages_per_step + 3]
    m_sc, l_sc, acc_sc = rest[pages_per_step + 3 :]
    step = pl.program_id(1)
    cached_count = meta_ref[0]
    member = meta_ref[1]
    source = meta_ref[2]

    @pl.when(step == 0)
    def _():
        m_sc[...] = jnp.full(m_sc.shape, masked_score, jnp.float32)
        l_sc[...] = jnp.zeros(l_sc.shape, jnp.float32)
        acc_sc[...] = jnp.zeros(acc_sc.shape, jnp.float32)

    def update(kv_pairs, page_flags, masks):
        q = q_ref[...]
        scores = []
        tops = []
        for (k, _), flag, mask in zip(kv_pairs, page_flags, masks):
            s = lax.dot_general(q, k, (((1,), (0,)), ((), ())), preferred_element_type=jnp.float32)
            if mask is not None:
                s = jnp.where(mask, s, masked_score)
            top = jnp.max(s, axis=1, keepdims=True)
            if flag is not None:
                top = jnp.where(flag, top, masked_score)
            scores.append(s)
            tops.append(top)
        m_prev = m_sc[...]
        m_new = m_prev
        for top in tops:
            m_new = jnp.maximum(m_new, top)
        alpha = jnp.exp((m_prev - m_new) * scale)
        l_new = alpha * l_sc[...]
        acc = alpha * acc_sc[...]
        for s, (_, v), flag, mask in zip(scores, kv_pairs, page_flags, masks):
            p = jnp.exp((s - m_new) * scale)
            if mask is not None:
                p = jnp.where(mask, p, 0.0)
            row_sum = jnp.sum(p, axis=1, keepdims=True)
            term = lax.dot_general(
                p.astype(jnp.bfloat16), v, (((1,), (1,)), ((), ())), preferred_element_type=jnp.float32
            )
            if flag is not None:
                row_sum = jnp.where(flag, row_sum, 0.0)
                term = jnp.where(flag, term, 0.0)
            l_new = l_new + row_sum
            acc = acc + term
        m_sc[...] = m_new
        l_sc[...] = l_new
        acc_sc[...] = acc

    cached_pairs = [(ref[0], ref[1]) for ref in pool_refs]
    first_page = step * pages_per_step

    @pl.when((step < cached_steps) & (first_page < cached_count))
    def _():
        flags = [first_page + i < cached_count for i in range(pages_per_step)]
        update(cached_pairs, flags, [None] * pages_per_step)

    fresh_pages = fresh_ref.shape[0]
    fresh_pairs = [(fresh_ref[e, 0], fresh_ref[e, 1]) for e in range(fresh_pages)]
    is_fresh = step == cached_steps

    @pl.when(is_fresh & (source >= member))
    def _():
        rows = q_ref.shape[0]
        row_tok = lax.broadcasted_iota(jnp.int32, (rows, PAGE), 0) // rows_per_tok
        col = lax.broadcasted_iota(jnp.int32, (rows, PAGE), 1)
        offset = (source - member) * tok_count
        masks = [e * PAGE + col <= row_tok + offset for e in range(fresh_pages)]
        update(fresh_pairs, [None] * fresh_pages, masks)

    @pl.when(is_fresh)
    def _():
        total = l_sc[...]
        filled = total > 0.0
        safe = jnp.where(filled, total, 1.0)
        o_ref[...] = (acc_sc[...] / safe).astype(o_ref.dtype)
        lse = jnp.where(filled, m_sc[...] * scale + jnp.log(safe), masked_score)
        wide = jnp.transpose(jnp.broadcast_to(lse, (lse.shape[0], 128)))
        lse_ref[...] = wide[0:1, :]


def partial_attention(q_block, kv_pool, fresh, slots, meta, cached_steps, head0, kv_heads):
    _, rows, head_dim = q_block.shape
    pages_per_step = PAGES_PER_STEP
    fresh_pages = fresh.shape[0]
    tok_count = fresh_pages * PAGE
    rows_per_tok = rows // tok_count
    scale = head_dim ** (-0.5)

    def pool_map(i):
        def index_map(h, j, slots_ref, meta_ref):
            jj = jnp.minimum(j, cached_steps - 1)
            idx = jnp.minimum(jj * pages_per_step + i, jnp.maximum(meta_ref[0] - 1, 0))
            return (slots_ref[idx], 0, h + head0, 0, 0)

        return index_map

    q_spec = pl.BlockSpec((None, rows, head_dim), lambda h, j, s, m: (h + head0, 0, 0))
    pool_specs = [
        pl.BlockSpec((None, 2, None, head_dim, PAGE), pool_map(i)) for i in range(pages_per_step)
    ]
    fresh_spec = pl.BlockSpec(
        (fresh_pages, 2, None, head_dim, PAGE), lambda h, j, s, m: (0, 0, h + head0, 0, 0)
    )
    o_spec = pl.BlockSpec((None, rows, head_dim), lambda h, j, s, m: (h, 0, 0))
    lse_spec = pl.BlockSpec((None, 1, rows), lambda h, j, s, m: (h, 0, 0))
    kernel = functools.partial(
        partial_kernel,
        pages_per_step=pages_per_step,
        cached_steps=cached_steps,
        rows_per_tok=rows_per_tok,
        tok_count=tok_count,
        scale=scale,
    )
    keys_per_row = cached_steps * pages_per_step * PAGE + tok_count
    cost = pl.CostEstimate(
        flops=4 * kv_heads * rows * keys_per_row * head_dim,
        transcendentals=kv_heads * rows * keys_per_row,
        bytes_accessed=kv_heads * (rows * head_dim * 6 + keys_per_row * head_dim * 4),
    )
    return pl.pallas_call(
        kernel,
        grid_spec=pltpu.PrefetchScalarGridSpec(
            num_scalar_prefetch=2,
            grid=(kv_heads, cached_steps + 1),
            in_specs=[q_spec] + pool_specs + [fresh_spec],
            out_specs=[o_spec, lse_spec],
            scratch_shapes=[
                pltpu.VMEM((rows, 1), jnp.float32),
                pltpu.VMEM((rows, 1), jnp.float32),
                pltpu.VMEM((rows, head_dim), jnp.float32),
            ],
        ),
        out_shape=[
            jax.ShapeDtypeStruct((kv_heads, rows, head_dim), jnp.bfloat16),
            jax.ShapeDtypeStruct((kv_heads, 1, rows), jnp.float32),
        ],
        compiler_params=pltpu.CompilerParams(dimension_semantics=("arbitrary", "arbitrary")),
        cost_estimate=cost,
    )(slots, meta, q_block, *([kv_pool] * pages_per_step), fresh)


def layer(tokens, norm_gain, w_query, w_key, w_value, w_out, kv_pool, cache_lengths, page_table):
    seq_position = lax.axis_index("seq")
    member = seq_position % GROUP
    group_id = seq_position // GROUP
    length = cache_lengths[group_id]
    first_new = length // PAGE
    table_row = page_table[group_id]
    tok_count = tokens.shape[0]
    kv_heads = w_key.shape[1] // HD
    q_heads = w_query.shape[1] // HD
    group_size = q_heads // kv_heads
    tok_pages = tok_count // PAGE
    cached_per_member = MAXLEN // PAGE // GROUP
    cached_steps = cached_per_member // PAGES_PER_STEP

    tp_size = lax.axis_size("tp")
    tp_index = lax.axis_index("tp")
    width = tokens.shape[1]
    remote = tp_swap(tokens, 2)
    both = tp_swap(jnp.stack([tokens, remote]), 1)
    whole = jnp.zeros((tok_count, width * tp_size), tokens.dtype)
    for index, piece in ((0, tokens), (2, remote), (1, both[0]), (3, both[1])):
        whole = lax.dynamic_update_slice(whole, piece, (0, (tp_index ^ index) * width))
    rows_float = whole.astype(jnp.float32)
    normed = (
        rows_float
        * lax.rsqrt(jnp.mean(rows_float * rows_float, axis=-1, keepdims=True) + norm_eps)
        * norm_gain.astype(jnp.float32)
    ).astype(jnp.bfloat16)
    positions = length + member * tok_count + jnp.arange(tok_count, dtype=jnp.int32)
    query_rows = jnp.dot(normed, w_query, preferred_element_type=jnp.float32).reshape(
        tok_count, q_heads, HD
    )
    query = (
        rotate(query_rows, positions)
        .astype(jnp.bfloat16)
        .reshape(tok_count, kv_heads, group_size, HD)
    )
    key_rows = jnp.dot(normed, w_key, preferred_element_type=jnp.float32).reshape(
        tok_count, kv_heads, HD
    )
    new_keys = rotate(key_rows, positions).astype(jnp.bfloat16)
    new_values = (
        jnp.dot(normed, w_value, preferred_element_type=jnp.float32)
        .astype(jnp.bfloat16)
        .reshape(tok_count, kv_heads, HD)
    )
    key_pages = new_keys.reshape(tok_pages, PAGE, kv_heads, HD).transpose(0, 2, 3, 1)
    value_pages = new_values.reshape(tok_pages, PAGE, kv_heads, HD).transpose(0, 2, 3, 1)
    fresh_local = jnp.stack([key_pages, value_pages], axis=1)

    q_own = query.transpose(1, 0, 2, 3).reshape(kv_heads, tok_count * group_size, HD)
    q_blocks = [q_own]
    for s in range(1, GROUP):
        q_blocks.append(group_shift(q_own, "seq", s))
    fresh_all = [fresh_local]
    for s in range(1, GROUP):
        fresh_all.append(group_shift(fresh_local, "seq", s))

    slots = table_row[member + GROUP * jnp.arange(cached_per_member, dtype=jnp.int32)]
    cached_count = jnp.maximum((first_new - member + GROUP - 1) // GROUP, 0)
    o_list = [None] * GROUP
    lse_list = [None] * GROUP
    own_o, own_lse = [], []
    for b, head0, n_heads in call_plan(kv_heads):
        source = (member - b) % GROUP
        meta = jnp.stack([cached_count, member, source]).astype(jnp.int32)
        o_b, lse_b = partial_attention(
            q_blocks[b], kv_pool, fresh_local, slots, meta, cached_steps, head0, n_heads
        )
        if b:
            o_list[b] = group_shift(o_b, "seq", GROUP - b)
            lse_list[b] = group_shift(lse_b, "seq", GROUP - b)
        else:
            own_o.append(o_b)
            own_lse.append(lse_b)
    o_list[0] = jnp.concatenate(own_o, axis=0)
    lse_list[0] = jnp.concatenate(own_lse, axis=0)
    lse_list = [x.reshape(kv_heads, -1, 1) for x in lse_list]
    lse_top = lse_list[0]
    for x in lse_list[1:]:
        lse_top = jnp.maximum(lse_top, x)
    weights = [jnp.exp(x - lse_top) for x in lse_list]
    weight_total = weights[0]
    for w in weights[1:]:
        weight_total = weight_total + w
    combined = weights[0] * o_list[0].astype(jnp.float32)
    for w, o in zip(weights[1:], o_list[1:]):
        combined = combined + w * o.astype(jnp.float32)
    combined = combined / weight_total
    attended = (
        combined.reshape(kv_heads, tok_count, group_size, HD)
        .transpose(1, 0, 2, 3)
        .reshape(tok_count, q_heads * HD)
        .astype(jnp.bfloat16)
    )
    out_blocks = jnp.einsum(
        "tk,kcn->ctn",
        attended,
        w_out.reshape(w_out.shape[0], tp_size, -1),
        preferred_element_type=jnp.float32,
    ).astype(jnp.bfloat16)

    def block(index):
        return lax.dynamic_index_in_dim(out_blocks, tp_index ^ index, 0, keepdims=False)

    near = tp_swap(jnp.stack([block(1), block(3)]), 1).astype(jnp.float32)
    own = block(0).astype(jnp.float32) + near[0]
    far = (block(2).astype(jnp.float32) + near[1]).astype(jnp.bfloat16)
    summed = own + tp_swap(far, 2).astype(jnp.float32)
    hidden = (tokens.astype(jnp.float32) + summed).astype(jnp.bfloat16)

    fresh_stack = jnp.stack(fresh_all)
    start_offset = (member - first_new) % GROUP
    new_pool = kv_pool
    for extra in range(2):
        page_id = start_offset + GROUP * extra
        source = page_id // tok_pages
        shift_id = (member - source) % GROUP
        page_piece = fresh_stack[shift_id, page_id % tok_pages]
        slot_id = table_row[first_new + page_id]
        new_pool = lax.dynamic_update_slice_in_dim(new_pool, page_piece[None], slot_id, 0)
    return (hidden, new_pool)


def call_plan(kv_heads):
    half = kv_heads // 2
    plan = [(0, 0, half)]
    plan += [(b, 0, kv_heads) for b in range(1, GROUP)]
    plan += [(0, half, kv_heads - half)]
    return plan


def solution(mesh):
    return jax.shard_map(
        layer,
        mesh=mesh,
        in_specs=(
            P("seq", "tp"),
            P(),
            P(None, "tp"),
            P(None, "tp"),
            P(None, "tp"),
            P("tp", None),
            P("seq", None, "tp", None, None),
            P(),
            P(),
        ),
        out_specs=(P("seq", "tp"), P("seq", None, "tp", None, None)),
        check_vma=False,
    )
```
